32 devices in a mesh: bl: 4 (over y, x), freq: 8 (over z, core).
Axes of the slice: x: 2, y: 2, z: 4, core: 2. Of those that a mesh axis runs over, the one named last changes fastest.
Arguments:
- visibility: bfloat16 [2, 64, 1024, 4096], P(None, None, 'freq', 'bl'), may hold values from -6 to 6
- mode_index: int32 [256], replicated, may hold values from 0 to 2047
- beam_mode_weights: bfloat16 [256, 64, 64], replicated, may hold values from -0.75 to 0.75
- inverse_cov: float32 [256, 1024, 1024], P(('bl', 'freq')), may hold values from -2 to 3, as said below
- noise_power: float32 [256, 1024], P(('bl', 'freq')), may hold values from 0.2 to 2
Outputs:
- filtered: float32 [256, 1024, 128], P(('bl', 'freq'))
The draws below stay inside these ranges and needn't reach their ends.
Inputs may be any that keep to these rules, and one draw needn't show every extreme that they name: Each inverse_cov[m] is symmetric positive definite.
All inputs are finite; a program needn't handle non-finite values.
Results may differ from the reference program's by a relative error of at most 0.0023.
Values may be sent and summed in bfloat16 or wider, within the bound.
No kernel may reach another device: no remote copies, remote signals or barrier semaphores. Data moves between devices by JAX's collectives and lax.ppermute only.
A program may use at most 192 MiB of HBM per device.

```python
import math
import jax
import jax.numpy as jnp
from jax import lax

SIDEREAL_SAMPLES = 4096
FREQUENCY_COUNT = 1024
WINDOW_MODES = 256
BASELINE_TOTAL = 64
RETAINED_MODES = 64


def draw_inverse_cov(key, part):
    keys = jax.random.split(jax.random.fold_in(key, 11), 4)
    smooth_amp = jnp.exp(jax.random.uniform(keys[0], (WINDOW_MODES, FREQUENCY_COUNT), jnp.float32, math.log(0.5), math.log(1.5)))
    rough_amp = jnp.exp(jax.random.uniform(keys[1], (WINDOW_MODES, FREQUENCY_COUNT), jnp.float32, math.log(0.5), math.log(1.5)))
    reach_top = FREQUENCY_COUNT / 8.0
    smooth_reach = jnp.exp(jax.random.uniform(keys[2], (WINDOW_MODES,), jnp.float32, math.log(2.0), math.log(reach_top)))
    rough_reach = jnp.exp(jax.random.uniform(keys[3], (WINDOW_MODES,), jnp.float32, 0.0, math.log(3.0)))
    positions = jnp.arange(FREQUENCY_COUNT, dtype=jnp.int32)
    gap_steps = jnp.abs(positions[:, None] - positions[None, :])
    gaps = gap_steps.astype(jnp.float32)
    parity = 1.0 - 2.0 * (gap_steps % 2).astype(jnp.float32)

    def one_mode(operands):
        first_amp, second_amp, first_reach, second_reach = operands
        smooth = first_amp[:, None] * first_amp[None, :] * jnp.exp(-gaps / first_reach)
        rough = second_amp[:, None] * second_amp[None, :] * parity * jnp.exp(-gaps / second_reach)
        return 0.5 * (smooth + rough)
    return lax.map(one_mode, (smooth_amp, rough_amp, smooth_reach, rough_reach))


def touch_ends(drawn, own_key, low, top_value):
    longest = drawn.shape.index(max(drawn.shape))
    spots = []
    for shift in (0, 1):
        where = [jax.random.randint(jax.random.fold_in(own_key, axis), (), 0, length) for axis, length in enumerate(drawn.shape)]
        where[longest] = (where[longest] + shift) % drawn.shape[longest]
        spots.append(tuple(where))
    return drawn.at[spots[0]].set(low).at[spots[1]].set(top_value)


def level_of(own_key, dims, cuts, low, top_value):
    loudness, own = 1.0, jax.random.fold_in(own_key, 6)
    for position, shards_of in cuts:
        heights = jnp.exp(jax.random.uniform(jax.random.fold_in(own, position), (shards_of,), jnp.float32, low / len(cuts), top_value / len(cuts)))
        loudness = loudness * jnp.repeat(heights, dims[position] // shards_of).reshape([-1 if axis == position else 1 for axis in range(len(dims))])
    return loudness


def noise(own_key, extent, spread, most, cuts=(), held_as=jnp.bfloat16):
    entries = spread * jax.random.normal(own_key, extent, jnp.float32)
    if cuts:
        entries = entries * level_of(own_key, extent, cuts, -0.22, 0.18)
    return jnp.clip(entries, -most, most).astype(held_as)


def setup_inputs(seed: int = 0) -> dict:
    key_of = jax.random.split(jax.random.key(seed), 6)
    visibility = noise(key_of[0], (2, BASELINE_TOTAL, FREQUENCY_COUNT, SIDEREAL_SAMPLES), 1.0, 6.0, ((2, 8), (3, 4)))
    mode_index = touch_ends(jax.random.randint(key_of[1], (WINDOW_MODES,), 0, SIDEREAL_SAMPLES // 2), jax.random.fold_in(key_of[1], 1), 0, (SIDEREAL_SAMPLES // 2) - 1).astype(jnp.int32)
    beam_mode_weights = noise(key_of[2], (WINDOW_MODES, RETAINED_MODES, BASELINE_TOTAL), BASELINE_TOTAL ** -0.5, 0.75)
    inverse_cov = draw_inverse_cov(jax.random.fold_in(key_of[5], 71), 0)
    noise_power = jnp.clip(jnp.exp(math.log(2.0) - 2.3025851 * jax.random.uniform(key_of[4], (WINDOW_MODES, FREQUENCY_COUNT), jnp.float32) ** level_of(key_of[4], (WINDOW_MODES, FREQUENCY_COUNT), ((0, 32),), -0.2, 0.2)), 0.2, 2.0)
    return {"visibility": visibility, "mode_index": mode_index, "beam_mode_weights": beam_mode_weights, "inverse_cov": inverse_cov, "noise_power": noise_power}


def dft_table(mode_index, sample_ids, length):
    phase_steps = mode_index[None, :] * sample_ids[:, None] % length
    phases = phase_steps.astype(jnp.float32) * (2.0 * math.pi / length)
    norming = 1.0 / math.sqrt(length)
    cosine = jnp.cos(phases) * norming
    sine_part = jnp.sin(phases) * norming
    real_rows = jnp.concatenate([cosine, -sine_part], axis=1)
    imag_rows = jnp.concatenate([sine_part, cosine], axis=1)
    return jnp.stack([real_rows, imag_rows]).astype(jnp.bfloat16)

def project(spectrum, beam_rows):
    row_count, freq_count, column_total = spectrum.shape
    mode_count = column_total // 2
    halves = spectrum.reshape(row_count, freq_count, 2, mode_count)
    projected = jnp.einsum('bfcm,msb->mfcs', halves, beam_rows.astype(jnp.float32), precision=lax.Precision.HIGHEST)
    return projected.reshape(mode_count, freq_count, 2 * beam_rows.shape[1])

def weigh_one(inverse, noise_row, block_rows):
    weighted = jnp.dot(inverse, block_rows, precision=lax.Precision.HIGHEST)
    return block_rows - noise_row[:, None] * weighted

def reference(visibility, mode_index, beam_mode_weights, inverse_cov, noise_power):
    dft_weights = dft_table(mode_index, jnp.arange(SIDEREAL_SAMPLES, dtype=jnp.int32), SIDEREAL_SAMPLES).astype(jnp.float32)
    block_width = 64 if FREQUENCY_COUNT % 64 == 0 else FREQUENCY_COUNT

    def one_block(start):
        samples = lax.dynamic_slice_in_dim(visibility, start, block_width, 2).astype(jnp.float32)
        spectrum = lax.dot_general(samples, dft_weights, (((0, 3), (0, 1)), ((), ())), precision=lax.Precision.HIGHEST)
        return project(spectrum, beam_mode_weights)
    starts = jnp.arange(FREQUENCY_COUNT // block_width, dtype=jnp.int32) * block_width
    pieces = lax.map(one_block, starts)
    projected = jnp.transpose(pieces, (1, 0, 2, 3)).reshape(WINDOW_MODES, FREQUENCY_COUNT, 2 * RETAINED_MODES)

    def apply_one(operands):
        return weigh_one(operands[0], operands[1], operands[2])
    return lax.map(apply_one, (inverse_cov, noise_power, projected))
```

```python
import math

import jax
import jax.numpy as jnp
from jax import lax
from jax.sharding import PartitionSpec as P

CHUNKS = 4


def dft_table(mode_index, sample_ids, length):
    phase_steps = mode_index[None, :] * sample_ids[:, None] % length
    phases = phase_steps.astype(jnp.float32) * (2.0 * math.pi / length)
    norming = 1.0 / math.sqrt(length)
    cosine = jnp.cos(phases) * norming
    sine_part = jnp.sin(phases) * norming
    real_rows = jnp.concatenate([cosine, -sine_part], axis=1)
    imag_rows = jnp.concatenate([sine_part, cosine], axis=1)
    return jnp.stack([real_rows, imag_rows]).astype(jnp.bfloat16)


def transform(samples, dft_weights):
    return lax.dot_general(
        samples, dft_weights, (((0, 3), (0, 1)), ((), ())), preferred_element_type=jnp.float32
    )


def project(spectrum, beam_rows):
    row_count, freq_count, column_total = spectrum.shape
    mode_count = column_total // 2
    halves = spectrum.reshape(row_count, freq_count, 2, mode_count)
    high = halves.astype(jnp.bfloat16)
    low = (halves - high.astype(jnp.float32)).astype(jnp.bfloat16)
    dims = (((0,), (2,)), ((3,), (0,)))
    projected = lax.dot_general(high, beam_rows, dims, preferred_element_type=jnp.float32)
    projected = projected + lax.dot_general(low, beam_rows, dims, preferred_element_type=jnp.float32)
    return projected.reshape(mode_count, freq_count, 2 * beam_rows.shape[1])


def weigh_all(inverse_cov, noise_power, owner_modes):
    weighted = jnp.einsum("mfg,mgk->mfk", inverse_cov, owner_modes, precision=lax.Precision.HIGH)
    return owner_modes - noise_power[:, :, None] * weighted


def body(visibility, mode_index, beam_mode_weights, inverse_cov, noise_power):
    bl_devices = lax.axis_size("bl")
    freq_devices = lax.axis_size("freq")
    local_times = visibility.shape[3]
    total_times = local_times * bl_devices
    mode_total = mode_index.shape[0]
    owned = inverse_cov.shape[0]
    chunk_count = math.gcd(CHUNKS, owned)
    chunk = owned // chunk_count
    sample_ids = lax.axis_index("bl") * local_times + jnp.arange(local_times, dtype=jnp.int32)
    index_grid = mode_index.reshape(bl_devices, freq_devices, owned)
    beam_grid = beam_mode_weights.reshape((bl_devices, freq_devices, owned) + beam_mode_weights.shape[1:])
    pieces = []
    for step in range(chunk_count):
        lo = step * chunk
        modes = index_grid[:, :, lo:lo + chunk].reshape(-1)
        beams = beam_grid[:, :, lo:lo + chunk].reshape((-1,) + beam_mode_weights.shape[1:])
        dft_weights = dft_table(modes, sample_ids, total_times)
        partial_terms = project(transform(visibility, dft_weights), beams)
        summed_modes = lax.psum_scatter(partial_terms, "bl", scatter_dimension=0, tiled=True)
        owner_modes = lax.all_to_all(summed_modes, "freq", split_axis=0, concat_axis=1, tiled=True)
        pieces.append(
            weigh_all(inverse_cov[lo:lo + chunk], noise_power[lo:lo + chunk], owner_modes)
        )
    return jnp.concatenate(pieces, axis=0)


def solution(mesh):
    placed = (
        P(None, None, "freq", "bl"),
        P(),
        P(),
        P(("bl", "freq"), None, None),
        P(("bl", "freq"), None),
    )
    return jax.shard_map(
        body, mesh=mesh, in_specs=placed, out_specs=P(("bl", "freq"), None, None), check_vma=False
    )
```

```python
import math

import jax
import jax.numpy as jnp
from jax import lax
from jax.sharding import PartitionSpec as P

CHUNKS = 4


def dft_table(mode_index, sample_ids, length, chunk_count):
    phase_steps = mode_index[None, :] * sample_ids[:, None] % length
    phases = phase_steps.astype(jnp.float32) * (2.0 * math.pi / length)
    norming = 1.0 / math.sqrt(length)
    cosine = (jnp.cos(phases) * norming).reshape(sample_ids.shape[0], chunk_count, 1, -1)
    sine_part = (jnp.sin(phases) * norming).reshape(sample_ids.shape[0], chunk_count, 1, -1)
    real_rows = jnp.concatenate([cosine, -sine_part], axis=2)
    imag_rows = jnp.concatenate([sine_part, cosine], axis=2)
    table = jnp.stack([real_rows, imag_rows]).astype(jnp.bfloat16)
    return table.reshape(2, sample_ids.shape[0], -1)


def transform(samples, dft_weights):
    return lax.dot_general(
        samples, dft_weights, (((0, 3), (0, 1)), ((), ())), preferred_element_type=jnp.float32
    )


def project(spectrum, beam_rows):
    row_count, freq_count, column_total = spectrum.shape
    mode_count = column_total // 2
    halves = spectrum.reshape(row_count, freq_count, 2, mode_count)
    high = lax.reduce_precision(halves, exponent_bits=8, mantissa_bits=7)
    low = (halves - high).astype(jnp.bfloat16)
    high = high.astype(jnp.bfloat16)
    dims = (((0,), (2,)), ((3,), (0,)))
    projected = lax.dot_general(high, beam_rows, dims, preferred_element_type=jnp.float32)
    projected = projected + lax.dot_general(low, beam_rows, dims, preferred_element_type=jnp.float32)
    return projected.reshape(mode_count, freq_count, 2 * beam_rows.shape[1])


def reduce_over_bl(partial, bl_devices):
    bits = bl_devices.bit_length() - 1
    if bits == 0 or (1 << bits) != bl_devices or partial.shape[1] % 2:
        return lax.psum_scatter(partial, "bl", scatter_dimension=0, tiled=True)
    me = lax.axis_index("bl")
    rows, freq_count = partial.shape[0], partial.shape[1]
    grid = partial.reshape((2,) * bits + (rows // bl_devices,) + partial.shape[1:])
    half = freq_count // 2
    parts = [grid[..., :half, :], grid[..., half:, :]]
    orders = [list(range(bits)), list(reversed(range(bits)))]
    axis_bits = [[bits - 1 - a for a in range(bits)] for _ in parts]
    for step in range(bits):
        for p in range(len(parts)):
            bit = orders[p][step]
            axis = axis_bits[p].index(bit)
            mine = (me >> bit) & 1
            keep = lax.dynamic_index_in_dim(parts[p], mine, axis, keepdims=False)
            send = lax.dynamic_index_in_dim(parts[p], 1 - mine, axis, keepdims=False)
            pairs = [(q, q ^ (1 << bit)) for q in range(bl_devices)]
            parts[p] = keep + lax.ppermute(send, "bl", perm=pairs)
            axis_bits[p].pop(axis)
    return jnp.concatenate(parts, axis=1)


def weigh_all(inverse_cov, noise_power, owner_modes):
    weighted = jnp.einsum("mfg,mgk->mfk", inverse_cov, owner_modes, precision=lax.Precision.HIGH)
    return owner_modes - noise_power[:, :, None] * weighted


def body(visibility, mode_index, beam_mode_weights, inverse_cov, noise_power):
    bl_devices = lax.axis_size("bl")
    freq_devices = lax.axis_size("freq")
    local_times = visibility.shape[3]
    total_times = local_times * bl_devices
    owned = inverse_cov.shape[0]
    chunk_count = math.gcd(CHUNKS, owned)
    chunk = owned // chunk_count
    sample_ids = lax.axis_index("bl") * local_times + jnp.arange(local_times, dtype=jnp.int32)
    index_grid = mode_index.reshape(bl_devices, freq_devices, chunk_count, chunk)
    ordered_modes = jnp.transpose(index_grid, (2, 0, 1, 3)).reshape(-1)
    beam_tail = beam_mode_weights.shape[1:]
    beam_grid = beam_mode_weights.reshape((bl_devices, freq_devices, chunk_count, chunk) + beam_tail)
    dft_weights = dft_table(ordered_modes, sample_ids, total_times, chunk_count)
    spectrum = transform(visibility, dft_weights)
    width = spectrum.shape[2] // chunk_count
    pieces = []
    for step in range(chunk_count):
        beams = beam_grid[:, :, step].reshape((-1,) + beam_tail)
        partial_terms = project(spectrum[:, :, step * width:(step + 1) * width], beams)
        summed_modes = reduce_over_bl(partial_terms, bl_devices)
        owner_modes = lax.all_to_all(summed_modes, "freq", split_axis=0, concat_axis=1, tiled=True)
        lo = step * chunk
        pieces.append(
            weigh_all(inverse_cov[lo:lo + chunk], noise_power[lo:lo + chunk], owner_modes)
        )
    return jnp.concatenate(pieces, axis=0)


def solution(mesh):
    placed = (
        P(None, None, "freq", "bl"),
        P(),
        P(),
        P(("bl", "freq"), None, None),
        P(("bl", "freq"), None),
    )
    return jax.shard_map(
        body, mesh=mesh, in_specs=placed, out_specs=P(("bl", "freq"), None, None), check_vma=False
    )
```

```python
import math

import jax
import jax.numpy as jnp
from jax import lax
from jax.sharding import PartitionSpec as P

CHUNKS = 4


def dft_table(mode_index, sample_ids, length, chunk_count):
    phase_steps = mode_index[None, :] * sample_ids[:, None] % length
    phases = phase_steps.astype(jnp.float32) * (2.0 * math.pi / length)
    norming = 1.0 / math.sqrt(length)
    cosine = (jnp.cos(phases) * norming).reshape(sample_ids.shape[0], chunk_count, 1, -1)
    sine_part = (jnp.sin(phases) * norming).reshape(sample_ids.shape[0], chunk_count, 1, -1)
    real_rows = jnp.concatenate([cosine, -sine_part], axis=2)
    imag_rows = jnp.concatenate([sine_part, cosine], axis=2)
    table = jnp.stack([real_rows, imag_rows]).astype(jnp.bfloat16)
    return table.reshape(2, sample_ids.shape[0], -1)


def transform(samples, dft_weights):
    return lax.dot_general(
        samples, dft_weights, (((0, 3), (0, 1)), ((), ())), preferred_element_type=jnp.float32
    )


def project(spectrum, beam_rows):
    row_count, freq_count, column_total = spectrum.shape
    mode_count = column_total // 2
    halves = spectrum.reshape(row_count, freq_count, 2, mode_count)
    high = lax.reduce_precision(halves, exponent_bits=8, mantissa_bits=7)
    low = (halves - high).astype(jnp.bfloat16)
    high = high.astype(jnp.bfloat16)
    dims = (((0,), (2,)), ((3,), (0,)))
    projected = lax.dot_general(high, beam_rows, dims, preferred_element_type=jnp.float32)
    projected = projected + lax.dot_general(low, beam_rows, dims, preferred_element_type=jnp.float32)
    return projected


def reduce_over_bl(partial, bl_devices):
    bits = bl_devices.bit_length() - 1
    rows = partial.shape[0]
    grid = partial.reshape((2,) * bits + (rows // bl_devices,) + partial.shape[1:])
    parts = [grid[..., 0:1, :], grid[..., 1:2, :]]
    orders = [list(range(bits)), list(reversed(range(bits)))]
    axis_bits = [[bits - 1 - a for a in range(bits)] for _ in parts]
    for step in range(bits):
        for p in range(len(parts)):
            bit = orders[p][step]
            axis = axis_bits[p].index(bit)
            keep = lax.index_in_dim(parts[p], 0, axis, keepdims=False)
            send = lax.index_in_dim(parts[p], 1, axis, keepdims=False)
            pairs = [(q, q ^ (1 << bit)) for q in range(bl_devices)]
            parts[p] = keep + lax.ppermute(send, "bl", perm=pairs)
            axis_bits[p].pop(axis)
    return jnp.concatenate(parts, axis=2)


def weigh_all(inverse_cov, noise_power, owner_modes):
    weighted = jnp.einsum("mfg,mgcs->mfcs", inverse_cov, owner_modes, precision=lax.Precision.HIGH)
    return owner_modes - noise_power[:, :, None, None] * weighted


def body(visibility, mode_index, beam_mode_weights, inverse_cov, noise_power):
    bl_devices = lax.axis_size("bl")
    freq_devices = lax.axis_size("freq")
    local_times = visibility.shape[3]
    total_times = local_times * bl_devices
    owned = inverse_cov.shape[0]
    chunk_count = math.gcd(CHUNKS, owned)
    chunk = owned // chunk_count
    me = lax.axis_index("bl")
    sample_ids = me * local_times + jnp.arange(local_times, dtype=jnp.int32)
    owners = jnp.bitwise_xor(me, jnp.arange(bl_devices, dtype=jnp.int32))
    index_grid = jnp.take(mode_index.reshape(bl_devices, freq_devices, chunk_count, chunk), owners, axis=0)
    ordered_modes = jnp.transpose(index_grid, (2, 0, 1, 3)).reshape(-1)
    beam_tail = beam_mode_weights.shape[1:]
    beam_grid = jnp.take(
        beam_mode_weights.reshape((bl_devices, freq_devices, chunk_count, chunk) + beam_tail), owners, axis=0
    )
    dft_weights = dft_table(ordered_modes, sample_ids, total_times, chunk_count)
    spectrum = transform(visibility, dft_weights)
    width = spectrum.shape[2] // chunk_count
    pieces = []
    for step in range(chunk_count):
        beams = beam_grid[:, :, step].reshape((-1,) + beam_tail)
        partial_terms = project(spectrum[:, :, step * width:(step + 1) * width], beams)
        summed_modes = reduce_over_bl(partial_terms, bl_devices)
        if pieces:
            summed_modes, pieces[-1] = lax.optimization_barrier((summed_modes, pieces[-1]))
        owner_modes = lax.all_to_all(summed_modes, "freq", split_axis=0, concat_axis=1, tiled=True)
        lo = step * chunk
        pieces.append(
            weigh_all(inverse_cov[lo:lo + chunk], noise_power[lo:lo + chunk], owner_modes)
        )
    filtered = jnp.concatenate(pieces, axis=0)
    return filtered.reshape(filtered.shape[:2] + (-1,))


def solution(mesh):
    placed = (
        P(None, None, "freq", "bl"),
        P(),
        P(),
        P(("bl", "freq"), None, None),
        P(("bl", "freq"), None),
    )
    return jax.shard_map(
        body, mesh=mesh, in_specs=placed, out_specs=P(("bl", "freq"), None, None), check_vma=False
    )
```

```python
import math

import jax
import jax.numpy as jnp
from jax import lax
from jax.sharding import PartitionSpec as P

def dft_table(mode_index, sample_ids, length, sizes):
    phase_steps = mode_index[None, :] * sample_ids[:, None] % length
    phases = phase_steps.astype(jnp.float32) * (2.0 * math.pi / length)
    norming = 1.0 / math.sqrt(length)
    cosine = jnp.cos(phases) * norming
    sine_part = jnp.sin(phases) * norming
    real_cols, imag_cols = [], []
    start = 0
    for size in sizes:
        cos_q, sin_q = cosine[:, start:start + size], sine_part[:, start:start + size]
        real_cols += [cos_q, -sin_q]
        imag_cols += [sin_q, cos_q]
        start += size
    real_rows = jnp.concatenate(real_cols, axis=1)
    imag_rows = jnp.concatenate(imag_cols, axis=1)
    return jnp.stack([real_rows, imag_rows]).astype(jnp.bfloat16)


def chunk_sizes(owned):
    if owned >= 4 and owned % 2 == 0:
        return [2] * (owned // 2 - 1) + [1, 1]
    return [1] * owned


def transform(samples, dft_weights):
    return lax.dot_general(
        samples, dft_weights, (((0, 3), (0, 1)), ((), ())), preferred_element_type=jnp.float32
    )


def project(spectrum, beam_rows):
    row_count, freq_count, column_total = spectrum.shape
    mode_count = column_total // 2
    halves = spectrum.reshape(row_count, freq_count, 2, mode_count)
    high = lax.reduce_precision(halves, exponent_bits=8, mantissa_bits=7)
    low = (halves - high).astype(jnp.bfloat16)
    high = high.astype(jnp.bfloat16)
    dims = (((0,), (2,)), ((3,), (0,)))
    projected = lax.dot_general(high, beam_rows, dims, preferred_element_type=jnp.float32)
    projected = projected + lax.dot_general(low, beam_rows, dims, preferred_element_type=jnp.float32)
    return projected


def reduce_over_bl(partial, bl_devices):
    bits = bl_devices.bit_length() - 1
    rows = partial.shape[0]
    grid = partial.reshape((2,) * bits + (rows // bl_devices,) + partial.shape[1:])
    parts = [grid[..., 0:1, :], grid[..., 1:2, :]]
    orders = [list(range(bits)), list(reversed(range(bits)))]
    axis_bits = [[bits - 1 - a for a in range(bits)] for _ in parts]
    for step in range(bits):
        for p in range(len(parts)):
            bit = orders[p][step]
            axis = axis_bits[p].index(bit)
            keep = lax.index_in_dim(parts[p], 0, axis, keepdims=False)
            send = lax.index_in_dim(parts[p], 1, axis, keepdims=False)
            pairs = [(q, q ^ (1 << bit)) for q in range(bl_devices)]
            parts[p] = keep + lax.ppermute(send, "bl", perm=pairs)
            axis_bits[p].pop(axis)
    return jnp.concatenate(parts, axis=2)


def weigh_all(inverse_cov, noise_power, owner_modes):
    weighted = jnp.einsum("mfg,mgcs->mfcs", inverse_cov, owner_modes, precision=lax.Precision.HIGH)
    return owner_modes - noise_power[:, :, None, None] * weighted


def body(visibility, mode_index, beam_mode_weights, inverse_cov, noise_power):
    bl_devices = lax.axis_size("bl")
    freq_devices = lax.axis_size("freq")
    local_times = visibility.shape[3]
    total_times = local_times * bl_devices
    owned = inverse_cov.shape[0]
    sizes = chunk_sizes(owned)
    me = lax.axis_index("bl")
    sample_ids = me * local_times + jnp.arange(local_times, dtype=jnp.int32)
    owners = jnp.bitwise_xor(me, jnp.arange(bl_devices, dtype=jnp.int32))
    order, start = [], 0
    for size in sizes:
        local = jnp.arange(freq_devices, dtype=jnp.int32)[:, None] * owned + start + jnp.arange(size, dtype=jnp.int32)
        order.append((owners[:, None, None] * (freq_devices * owned) + local[None]).reshape(-1))
        start += size
    order = jnp.concatenate(order)
    ordered_modes = jnp.take(mode_index, order, mode="clip")
    ordered_beams = jnp.take(beam_mode_weights, order, axis=0, mode="clip")
    dft_weights = dft_table(ordered_modes, sample_ids, total_times, [s * bl_devices * freq_devices for s in sizes])
    spectrum = transform(visibility, dft_weights)
    pieces = []
    start = 0
    previous = None
    for size in sizes:
        count = bl_devices * freq_devices * size
        columns = spectrum[:, :, 2 * start * bl_devices * freq_devices:][:, :, :2 * count]
        if previous is not None:
            columns, previous = lax.optimization_barrier((columns, previous))
        beams = ordered_beams[start * bl_devices * freq_devices:][:count]
        partial_terms = project(columns, beams)
        previous = partial_terms
        summed_modes = reduce_over_bl(partial_terms, bl_devices)
        if pieces:
            summed_modes, pieces[-1] = lax.optimization_barrier((summed_modes, pieces[-1]))
        owner_modes = lax.all_to_all(summed_modes, "freq", split_axis=0, concat_axis=1, tiled=True)
        pieces.append(
            weigh_all(inverse_cov[start:start + size], noise_power[start:start + size], owner_modes)
        )
        start += size
    filtered = jnp.concatenate(pieces, axis=0)
    return filtered.reshape(filtered.shape[:2] + (-1,))


def solution(mesh):
    placed = (
        P(None, None, "freq", "bl"),
        P(),
        P(),
        P(("bl", "freq"), None, None),
        P(("bl", "freq"), None),
    )
    return jax.shard_map(
        body, mesh=mesh, in_specs=placed, out_specs=P(("bl", "freq"), None, None), check_vma=False
    )
```

```python
import math

import jax
import jax.numpy as jnp
from jax import lax
from jax.sharding import PartitionSpec as P

def dft_table(mode_index, sample_ids, length, sizes):
    phase_steps = mode_index[None, :] * sample_ids[:, None] % length
    phases = phase_steps.astype(jnp.float32) * (2.0 * math.pi / length)
    norming = 1.0 / math.sqrt(length)
    cosine = jnp.cos(phases) * norming
    sine_part = jnp.sin(phases) * norming
    real_cols, imag_cols = [], []
    start = 0
    for size in sizes:
        cos_q, sin_q = cosine[:, start:start + size], sine_part[:, start:start + size]
        real_cols += [cos_q, -sin_q]
        imag_cols += [sin_q, cos_q]
        start += size
    real_rows = jnp.concatenate(real_cols, axis=1)
    imag_rows = jnp.concatenate(imag_cols, axis=1)
    return jnp.stack([real_rows, imag_rows]).astype(jnp.bfloat16)


def chunk_sizes(owned):
    if owned >= 4 and owned % 2 == 0:
        return [1] + [2] * (owned // 2 - 1) + [1]
    return [1] * owned


def transform(samples, dft_weights):
    return lax.dot_general(
        samples, dft_weights, (((0, 3), (0, 1)), ((), ())), preferred_element_type=jnp.float32
    )


def project(spectrum, beam_rows):
    row_count, freq_count, column_total = spectrum.shape
    mode_count = column_total // 2
    halves = spectrum.reshape(row_count, freq_count, 2, mode_count)
    high = lax.reduce_precision(halves, exponent_bits=8, mantissa_bits=7)
    low = (halves - high).astype(jnp.bfloat16)
    high = high.astype(jnp.bfloat16)
    dims = (((0,), (2,)), ((3,), (0,)))
    projected = lax.dot_general(high, beam_rows, dims, preferred_element_type=jnp.float32)
    projected = projected + lax.dot_general(low, beam_rows, dims, preferred_element_type=jnp.float32)
    return projected


def reduce_over_bl(partial, bl_devices, hold=None):
    bits = bl_devices.bit_length() - 1
    rows = partial.shape[0]
    grid = partial.reshape((2,) * bits + (rows // bl_devices,) + partial.shape[1:])
    parts = [grid[..., 0:1, :], grid[..., 1:2, :]]
    orders = [list(range(bits)), list(reversed(range(bits)))]
    axis_bits = [[bits - 1 - a for a in range(bits)] for _ in parts]
    for step in range(bits):
        for p in range(len(parts)):
            bit = orders[p][step]
            axis = axis_bits[p].index(bit)
            keep = lax.index_in_dim(parts[p], 0, axis, keepdims=False)
            send = lax.index_in_dim(parts[p], 1, axis, keepdims=False)
            pairs = [(q, q ^ (1 << bit)) for q in range(bl_devices)]
            parts[p] = keep + lax.ppermute(send, "bl", perm=pairs)
            axis_bits[p].pop(axis)
        if step == 0 and hold is not None:
            parts, hold = lax.optimization_barrier((parts, hold))
    return jnp.concatenate(parts, axis=2), hold


def weigh_all(inverse_cov, noise_power, owner_modes):
    weighted = jnp.einsum("mfg,mgcs->mfcs", inverse_cov, owner_modes, precision=lax.Precision.HIGH)
    return owner_modes - noise_power[:, :, None, None] * weighted


def body(visibility, mode_index, beam_mode_weights, inverse_cov, noise_power):
    bl_devices = lax.axis_size("bl")
    freq_devices = lax.axis_size("freq")
    local_times = visibility.shape[3]
    total_times = local_times * bl_devices
    owned = inverse_cov.shape[0]
    sizes = chunk_sizes(owned)
    me = lax.axis_index("bl")
    sample_ids = me * local_times + jnp.arange(local_times, dtype=jnp.int32)
    owners = jnp.bitwise_xor(me, jnp.arange(bl_devices, dtype=jnp.int32))
    order, start = [], 0
    for size in sizes:
        local = jnp.arange(freq_devices, dtype=jnp.int32)[:, None] * owned + start + jnp.arange(size, dtype=jnp.int32)
        order.append((owners[:, None, None] * (freq_devices * owned) + local[None]).reshape(-1))
        start += size
    order = jnp.concatenate(order)
    ordered_modes = jnp.take(mode_index, order, mode="clip")
    ordered_beams = jnp.take(beam_mode_weights, order, axis=0, mode="clip")
    dft_weights = dft_table(ordered_modes, sample_ids, total_times, [s * bl_devices * freq_devices for s in sizes])
    first_width = 2 * sizes[0] * bl_devices * freq_devices
    spectrum = None
    pieces = []
    start = 0
    for size in sizes:
        count = bl_devices * freq_devices * size
        if start == 0:
            columns = transform(visibility, dft_weights[:, :, :first_width])
        else:
            offset = 2 * start * bl_devices * freq_devices - first_width
            columns = spectrum[:, :, offset:offset + 2 * count]
        beams = ordered_beams[start * bl_devices * freq_devices:][:count]
        partial_terms = project(columns, beams)
        hold = dft_weights[:, :, first_width:] if start == 0 else None
        summed_modes, hold = reduce_over_bl(partial_terms, bl_devices, hold)
        if start == 0:
            spectrum = transform(visibility, hold)
        if pieces:
            summed_modes, pieces[-1] = lax.optimization_barrier((summed_modes, pieces[-1]))
        owner_modes = lax.all_to_all(summed_modes, "freq", split_axis=0, concat_axis=1, tiled=True)
        pieces.append(
            weigh_all(inverse_cov[start:start + size], noise_power[start:start + size], owner_modes)
        )
        start += size
    filtered = jnp.concatenate(pieces, axis=0)
    return filtered.reshape(filtered.shape[:2] + (-1,))


def solution(mesh):
    placed = (
        P(None, None, "freq", "bl"),
        P(),
        P(),
        P(("bl", "freq"), None, None),
        P(("bl", "freq"), None),
    )
    return jax.shard_map(
        body, mesh=mesh, in_specs=placed, out_specs=P(("bl", "freq"), None, None), check_vma=False
    )
```

```python
import math

import jax
import jax.numpy as jnp
from jax import lax
from jax.sharding import PartitionSpec as P

CHUNKS = 4


def dft_table(mode_index, sample_ids, length, chunk_count):
    phase_steps = mode_index[None, :] * sample_ids[:, None] % length
    phases = phase_steps.astype(jnp.float32) * (2.0 * math.pi / length)
    norming = 1.0 / math.sqrt(length)
    cosine = (jnp.cos(phases) * norming).reshape(sample_ids.shape[0], chunk_count, 1, -1)
    sine_part = (jnp.sin(phases) * norming).reshape(sample_ids.shape[0], chunk_count, 1, -1)
    real_rows = jnp.concatenate([cosine, -sine_part], axis=2)
    imag_rows = jnp.concatenate([sine_part, cosine], axis=2)
    table = jnp.stack([real_rows, imag_rows]).astype(jnp.bfloat16)
    return table.reshape(2, sample_ids.shape[0], -1)


def transform(samples, dft_weights):
    return lax.dot_general(
        samples, dft_weights, (((0, 3), (0, 1)), ((), ())), preferred_element_type=jnp.float32
    )


def project(spectrum, beam_rows):
    row_count, freq_count, column_total = spectrum.shape
    mode_count = column_total // 2
    halves = spectrum.reshape(row_count, freq_count, 2, mode_count)
    high = lax.reduce_precision(halves, exponent_bits=8, mantissa_bits=7)
    low = (halves - high).astype(jnp.bfloat16)
    high = high.astype(jnp.bfloat16)
    dims = (((0,), (2,)), ((3,), (0,)))
    projected = lax.dot_general(high, beam_rows, dims, preferred_element_type=jnp.float32)
    projected = projected + lax.dot_general(low, beam_rows, dims, preferred_element_type=jnp.float32)
    return projected


RESIDUAL_LEVELS = 7
RESIDUAL_SCALE = RESIDUAL_LEVELS * 256.0


def encode_pairs(block, axis):
    high = lax.reduce_precision(block, exponent_bits=8, mantissa_bits=7)
    size = jnp.abs(high)
    ratio = jnp.where(size > 0, (block - high) / jnp.where(size > 0, size, 1.0), 0.0)
    steps = jnp.clip(jnp.round(ratio * RESIDUAL_SCALE), -RESIDUAL_LEVELS, RESIDUAL_LEVELS)
    rows = block.shape[axis] // 2
    first = lax.slice_in_dim(steps, 0, rows, axis=axis)
    second = lax.slice_in_dim(steps, rows, 2 * rows, axis=axis)
    code = first * (2 * RESIDUAL_LEVELS + 1) + second
    return jnp.concatenate([high, code], axis=axis).astype(jnp.bfloat16)


def decode_pairs(payload, axis):
    rows = payload.shape[axis] // 3
    high = lax.slice_in_dim(payload, 0, 2 * rows, axis=axis).astype(jnp.float32)
    code = lax.slice_in_dim(payload, 2 * rows, 3 * rows, axis=axis).astype(jnp.float32)
    first = jnp.round(code / (2 * RESIDUAL_LEVELS + 1))
    second = code - first * (2 * RESIDUAL_LEVELS + 1)
    steps = jnp.concatenate([first, second], axis=axis)
    return high + jnp.abs(high) * (steps / RESIDUAL_SCALE)


def reduce_over_bl(partial, bl_devices):
    bits = bl_devices.bit_length() - 1
    rows = partial.shape[0]
    grid = partial.reshape((2,) * bits + (rows // bl_devices,) + partial.shape[1:])
    parts = [grid[..., 0:1, :], grid[..., 1:2, :]]
    orders = [list(range(bits)), list(reversed(range(bits)))]
    axis_bits = [[bits - 1 - a for a in range(bits)] for _ in parts]
    for step in range(bits):
        for p in range(len(parts)):
            bit = orders[p][step]
            axis = axis_bits[p].index(bit)
            keep = lax.index_in_dim(parts[p], 0, axis, keepdims=False)
            send = lax.index_in_dim(parts[p], 1, axis, keepdims=False)
            pairs = [(q, q ^ (1 << bit)) for q in range(bl_devices)]
            row_axis = len(axis_bits[p]) - 1
            if send.shape[row_axis] % 2 == 0:
                moved = lax.ppermute(encode_pairs(send, row_axis), "bl", perm=pairs)
                parts[p] = keep + decode_pairs(moved, row_axis)
            else:
                parts[p] = keep + lax.ppermute(send, "bl", perm=pairs)
            axis_bits[p].pop(axis)
    return jnp.concatenate(parts, axis=2)


def weigh_all(inverse_cov, noise_power, owner_modes):
    weighted = jnp.einsum("mfg,mgcs->mfcs", inverse_cov, owner_modes, precision=lax.Precision.HIGH)
    return owner_modes - noise_power[:, :, None, None] * weighted


def body(visibility, mode_index, beam_mode_weights, inverse_cov, noise_power):
    bl_devices = lax.axis_size("bl")
    freq_devices = lax.axis_size("freq")
    local_times = visibility.shape[3]
    total_times = local_times * bl_devices
    owned = inverse_cov.shape[0]
    chunk_count = math.gcd(CHUNKS, owned)
    chunk = owned // chunk_count
    me = lax.axis_index("bl")
    sample_ids = me * local_times + jnp.arange(local_times, dtype=jnp.int32)
    owners = jnp.bitwise_xor(me, jnp.arange(bl_devices, dtype=jnp.int32))
    index_grid = jnp.take(mode_index.reshape(bl_devices, freq_devices, chunk_count, chunk), owners, axis=0)
    ordered_modes = jnp.transpose(index_grid, (2, 0, 1, 3)).reshape(-1)
    beam_tail = beam_mode_weights.shape[1:]
    beam_grid = jnp.take(
        beam_mode_weights.reshape((bl_devices, freq_devices, chunk_count, chunk) + beam_tail), owners, axis=0
    )
    dft_weights = dft_table(ordered_modes, sample_ids, total_times, chunk_count)
    spectrum = transform(visibility, dft_weights)
    width = spectrum.shape[2] // chunk_count
    pieces = []
    for step in range(chunk_count):
        beams = beam_grid[:, :, step].reshape((-1,) + beam_tail)
        partial_terms = project(spectrum[:, :, step * width:(step + 1) * width], beams)
        summed_modes = reduce_over_bl(partial_terms, bl_devices)
        if pieces:
            summed_modes, pieces[-1] = lax.optimization_barrier((summed_modes, pieces[-1]))
        owner_modes = lax.all_to_all(summed_modes, "freq", split_axis=0, concat_axis=1, tiled=True)
        lo = step * chunk
        pieces.append(
            weigh_all(inverse_cov[lo:lo + chunk], noise_power[lo:lo + chunk], owner_modes)
        )
    filtered = jnp.concatenate(pieces, axis=0)
    return filtered.reshape(filtered.shape[:2] + (-1,))


def solution(mesh):
    placed = (
        P(None, None, "freq", "bl"),
        P(),
        P(),
        P(("bl", "freq"), None, None),
        P(("bl", "freq"), None),
    )
    return jax.shard_map(
        body, mesh=mesh, in_specs=placed, out_specs=P(("bl", "freq"), None, None), check_vma=False
    )
```

```python
import math

import jax
import jax.numpy as jnp
from jax import lax
from jax.sharding import PartitionSpec as P

CHUNKS = 4


def dft_table(mode_index, sample_ids, length, chunk_count):
    phase_steps = mode_index[None, :] * sample_ids[:, None] % length
    phases = phase_steps.astype(jnp.float32) * (2.0 * math.pi / length)
    norming = 1.0 / math.sqrt(length)
    cosine = (jnp.cos(phases) * norming).reshape(sample_ids.shape[0], chunk_count, 1, -1)
    sine_part = (jnp.sin(phases) * norming).reshape(sample_ids.shape[0], chunk_count, 1, -1)
    real_rows = jnp.concatenate([cosine, -sine_part], axis=2)
    imag_rows = jnp.concatenate([sine_part, cosine], axis=2)
    table = jnp.stack([real_rows, imag_rows]).astype(jnp.bfloat16)
    return table.reshape(2, sample_ids.shape[0], -1)


def transform(samples, dft_weights):
    return lax.dot_general(
        samples, dft_weights, (((0, 3), (0, 1)), ((), ())), preferred_element_type=jnp.float32
    )


def project(spectrum, beam_rows):
    row_count, freq_count, column_total = spectrum.shape
    mode_count = column_total // 2
    halves = spectrum.reshape(row_count, freq_count, 2, mode_count)
    high = lax.reduce_precision(halves, exponent_bits=8, mantissa_bits=7)
    low = (halves - high).astype(jnp.bfloat16)
    high = high.astype(jnp.bfloat16)
    dims = (((0,), (2,)), ((3,), (0,)))
    projected = lax.dot_general(high, beam_rows, dims, preferred_element_type=jnp.float32)
    projected = projected + lax.dot_general(low, beam_rows, dims, preferred_element_type=jnp.float32)
    return projected


RESIDUAL_LEVELS = 7
RESIDUAL_SCALE = RESIDUAL_LEVELS * 256.0


def encode_pairs(block, axis):
    high = lax.reduce_precision(block, exponent_bits=8, mantissa_bits=7)
    size = jnp.abs(high)
    ratio = jnp.where(size > 0, (block - high) / jnp.where(size > 0, size, 1.0), 0.0)
    steps = jnp.clip(jnp.round(ratio * RESIDUAL_SCALE), -RESIDUAL_LEVELS, RESIDUAL_LEVELS)
    rows = block.shape[axis] // 2
    first = lax.slice_in_dim(steps, 0, rows, axis=axis)
    second = lax.slice_in_dim(steps, rows, 2 * rows, axis=axis)
    code = first * (2 * RESIDUAL_LEVELS + 1) + second
    return jnp.concatenate([high, code], axis=axis).astype(jnp.bfloat16)


def decode_pairs(payload, axis):
    rows = payload.shape[axis] // 3
    high = lax.slice_in_dim(payload, 0, 2 * rows, axis=axis).astype(jnp.float32)
    code = lax.slice_in_dim(payload, 2 * rows, 3 * rows, axis=axis).astype(jnp.float32)
    first = jnp.round(code / (2 * RESIDUAL_LEVELS + 1))
    second = code - first * (2 * RESIDUAL_LEVELS + 1)
    steps = jnp.concatenate([first, second], axis=axis)
    return high + jnp.abs(high) * (steps / RESIDUAL_SCALE)


def split_for_bl(partial, bl_devices):
    bits = bl_devices.bit_length() - 1
    rows = partial.shape[0]
    grid = partial.reshape((2,) * bits + (rows // bl_devices,) + partial.shape[1:])
    return [[grid[..., 0:1, :], [bits - 1 - a for a in range(bits)]],
            [grid[..., 1:2, :], [bits - 1 - a for a in range(bits)]]]


def exchange_step(state, step, bl_devices):
    bits = bl_devices.bit_length() - 1
    orders = [list(range(bits)), list(reversed(range(bits)))]
    sends, keeps = [], []
    for p, (data, axis_bits) in enumerate(state):
        bit = orders[p][step]
        axis = axis_bits.index(bit)
        keeps.append((lax.index_in_dim(data, 0, axis, keepdims=False), axis_bits[:axis] + axis_bits[axis + 1:], bit))
        send = lax.index_in_dim(data, 1, axis, keepdims=False)
        row_axis = len(axis_bits) - 1
        sends.append(encode_pairs(send, row_axis) if send.shape[row_axis] % 2 == 0 else send)
    return sends, keeps


def fold_step(keeps, received):
    state = []
    for (keep, axis_bits, bit), moved in zip(keeps, received):
        row_axis = len(axis_bits)
        if moved.dtype == jnp.bfloat16:
            moved = decode_pairs(moved, row_axis)
        state.append([keep + moved, axis_bits])
    return state


def weigh_all(inverse_cov, noise_power, owner_modes):
    weighted = jnp.einsum("mfg,mgcs->mfcs", inverse_cov, owner_modes, precision=lax.Precision.HIGH)
    return owner_modes - noise_power[:, :, None, None] * weighted


def body(visibility, mode_index, beam_mode_weights, inverse_cov, noise_power):
    bl_devices = lax.axis_size("bl")
    freq_devices = lax.axis_size("freq")
    local_times = visibility.shape[3]
    total_times = local_times * bl_devices
    owned = inverse_cov.shape[0]
    chunk_count = math.gcd(CHUNKS, owned)
    chunk = owned // chunk_count
    me = lax.axis_index("bl")
    sample_ids = me * local_times + jnp.arange(local_times, dtype=jnp.int32)
    owners = jnp.bitwise_xor(me, jnp.arange(bl_devices, dtype=jnp.int32))
    index_grid = jnp.take(mode_index.reshape(bl_devices, freq_devices, chunk_count, chunk), owners, axis=0)
    ordered_modes = jnp.transpose(index_grid, (2, 0, 1, 3)).reshape(-1)
    beam_tail = beam_mode_weights.shape[1:]
    beam_grid = jnp.take(
        beam_mode_weights.reshape((bl_devices, freq_devices, chunk_count, chunk) + beam_tail), owners, axis=0
    )
    dft_weights = dft_table(ordered_modes, sample_ids, total_times, chunk_count)
    spectrum = transform(visibility, dft_weights)
    width = spectrum.shape[2] // chunk_count
    bits = bl_devices.bit_length() - 1
    states = []
    for step in range(chunk_count):
        beams = beam_grid[:, :, step].reshape((-1,) + beam_tail)
        partial_terms = project(spectrum[:, :, step * width:(step + 1) * width], beams)
        states.append(split_for_bl(partial_terms, bl_devices))
    pieces = []
    for slot in range(chunk_count + bits - 1):
        active = [(slot - t, t) for t in range(bits) if 0 <= slot - t < chunk_count]
        plans = [exchange_step(states[k], t, bl_devices) for k, t in active]
        flat = [payload for sends, _ in plans for payload in sends]
        flat = list(lax.optimization_barrier(tuple(flat)))
        for (k, t), (sends, keeps) in zip(active, plans):
            received = []
            for p in range(len(sends)):
                bit = keeps[p][2]
                pairs = [(q, q ^ (1 << bit)) for q in range(bl_devices)]
                received.append(lax.ppermute(flat.pop(0), "bl", perm=pairs))
            states[k] = fold_step(keeps, received)
            if t == bits - 1:
                summed_modes = jnp.concatenate([states[k][0][0], states[k][1][0]], axis=2)
                if pieces:
                    summed_modes, pieces[-1] = lax.optimization_barrier((summed_modes, pieces[-1]))
                owner_modes = lax.all_to_all(summed_modes, "freq", split_axis=0, concat_axis=1, tiled=True)
                lo = k * chunk
                pieces.append(
                    weigh_all(inverse_cov[lo:lo + chunk], noise_power[lo:lo + chunk], owner_modes)
                )
    filtered = jnp.concatenate(pieces, axis=0)
    return filtered.reshape(filtered.shape[:2] + (-1,))


def solution(mesh):
    placed = (
        P(None, None, "freq", "bl"),
        P(),
        P(),
        P(("bl", "freq"), None, None),
        P(("bl", "freq"), None),
    )
    return jax.shard_map(
        body, mesh=mesh, in_specs=placed, out_specs=P(("bl", "freq"), None, None), check_vma=False
    )
```

```python
import math

import jax
import jax.numpy as jnp
from jax import lax
from jax.sharding import PartitionSpec as P

CHUNKS = 4


def dft_table(mode_index, sample_ids, length, chunk_count):
    phase_steps = mode_index[None, :] * sample_ids[:, None] % length
    phases = phase_steps.astype(jnp.float32) * (2.0 * math.pi / length)
    norming = 1.0 / math.sqrt(length)
    cosine = (jnp.cos(phases) * norming).reshape(sample_ids.shape[0], chunk_count, 1, -1)
    sine_part = (jnp.sin(phases) * norming).reshape(sample_ids.shape[0], chunk_count, 1, -1)
    real_rows = jnp.concatenate([cosine, -sine_part], axis=2)
    imag_rows = jnp.concatenate([sine_part, cosine], axis=2)
    table = jnp.stack([real_rows, imag_rows]).astype(jnp.bfloat16)
    return table.reshape(2, sample_ids.shape[0], -1)


def transform(samples, dft_weights):
    return lax.dot_general(
        samples, dft_weights, (((0, 3), (0, 1)), ((), ())), preferred_element_type=jnp.float32
    )


def project(spectrum, beam_rows):
    row_count, freq_count, column_total = spectrum.shape
    mode_count = column_total // 2
    halves = spectrum.reshape(row_count, freq_count, 2, mode_count)
    high = lax.reduce_precision(halves, exponent_bits=8, mantissa_bits=7)
    low = (halves - high).astype(jnp.bfloat16)
    high = high.astype(jnp.bfloat16)
    dims = (((0,), (2,)), ((3,), (0,)))
    projected = lax.dot_general(high, beam_rows, dims, preferred_element_type=jnp.float32)
    projected = projected + lax.dot_general(low, beam_rows, dims, preferred_element_type=jnp.float32)
    return projected


RESIDUAL_LEVELS = 7
RESIDUAL_SCALE = RESIDUAL_LEVELS * 256.0


def encode_pairs(block, axis):
    high = lax.reduce_precision(block, exponent_bits=8, mantissa_bits=7)
    size = jnp.abs(high)
    ratio = jnp.where(size > 0, (block - high) / jnp.where(size > 0, size, 1.0), 0.0)
    steps = jnp.clip(jnp.round(ratio * RESIDUAL_SCALE), -RESIDUAL_LEVELS, RESIDUAL_LEVELS)
    rows = block.shape[axis] // 2
    first = lax.slice_in_dim(steps, 0, rows, axis=axis)
    second = lax.slice_in_dim(steps, rows, 2 * rows, axis=axis)
    code = first * (2 * RESIDUAL_LEVELS + 1) + second
    return jnp.concatenate([high, code], axis=axis).astype(jnp.bfloat16)


def decode_pairs(payload, axis):
    rows = payload.shape[axis] // 3
    high = lax.slice_in_dim(payload, 0, 2 * rows, axis=axis).astype(jnp.float32)
    code = lax.slice_in_dim(payload, 2 * rows, 3 * rows, axis=axis).astype(jnp.float32)
    first = jnp.round(code / (2 * RESIDUAL_LEVELS + 1))
    second = code - first * (2 * RESIDUAL_LEVELS + 1)
    steps = jnp.concatenate([first, second], axis=axis)
    return high + jnp.abs(high) * (steps / RESIDUAL_SCALE)


def split_for_bl(partial, bl_devices):
    bits = bl_devices.bit_length() - 1
    rows = partial.shape[0]
    grid = partial.reshape((2,) * bits + (rows // bl_devices,) + partial.shape[1:])
    return [[grid[..., 0:1, :], [bits - 1 - a for a in range(bits)]],
            [grid[..., 1:2, :], [bits - 1 - a for a in range(bits)]]]


def exchange_step(state, step, bl_devices):
    bits = bl_devices.bit_length() - 1
    orders = [list(range(bits)), list(reversed(range(bits)))]
    sends, keeps = [], []
    for p, (data, axis_bits) in enumerate(state):
        bit = orders[p][step]
        axis = axis_bits.index(bit)
        keeps.append((lax.index_in_dim(data, 0, axis, keepdims=False), axis_bits[:axis] + axis_bits[axis + 1:], bit))
        send = lax.index_in_dim(data, 1, axis, keepdims=False)
        row_axis = len(axis_bits) - 1
        sends.append(encode_pairs(send, row_axis) if send.shape[row_axis] % 2 == 0 else send)
    return sends, keeps


def fold_step(keeps, received):
    state = []
    for (keep, axis_bits, bit), moved in zip(keeps, received):
        row_axis = len(axis_bits)
        if moved.dtype == jnp.bfloat16:
            moved = decode_pairs(moved, row_axis)
        state.append([keep + moved, axis_bits])
    return state


def weigh_all(inverse_cov, noise_power, owner_modes):
    weighted = jnp.einsum("mfg,mgcs->mfcs", inverse_cov, owner_modes, precision=lax.Precision.HIGH)
    return owner_modes - noise_power[:, :, None, None] * weighted


def body(visibility, mode_index, beam_mode_weights, inverse_cov, noise_power):
    bl_devices = lax.axis_size("bl")
    freq_devices = lax.axis_size("freq")
    local_times = visibility.shape[3]
    total_times = local_times * bl_devices
    owned = inverse_cov.shape[0]
    chunk_count = math.gcd(CHUNKS, owned)
    chunk = owned // chunk_count
    me = lax.axis_index("bl")
    sample_ids = me * local_times + jnp.arange(local_times, dtype=jnp.int32)
    owners = jnp.bitwise_xor(me, jnp.arange(bl_devices, dtype=jnp.int32))
    index_grid = jnp.take(mode_index.reshape(bl_devices, freq_devices, chunk_count, chunk), owners, axis=0)
    ordered_modes = jnp.transpose(index_grid, (2, 0, 1, 3)).reshape(-1)
    beam_tail = beam_mode_weights.shape[1:]
    beam_grid = jnp.take(
        beam_mode_weights.reshape((bl_devices, freq_devices, chunk_count, chunk) + beam_tail), owners, axis=0
    )
    dft_weights = dft_table(ordered_modes, sample_ids, total_times, chunk_count)
    spectrum = transform(visibility, dft_weights)
    width = spectrum.shape[2] // chunk_count
    bits = bl_devices.bit_length() - 1
    states = []
    for step in range(chunk_count):
        beams = beam_grid[:, :, step].reshape((-1,) + beam_tail)
        partial_terms = project(spectrum[:, :, step * width:(step + 1) * width], beams)
        states.append(split_for_bl(partial_terms, bl_devices))
    pieces = []
    for slot in range(chunk_count + bits - 1):
        active = [(slot - t, t) for t in range(bits) if 0 <= slot - t < chunk_count]
        plans = [exchange_step(states[k], t, bl_devices) for k, t in active]
        flat = [payload for sends, _ in plans for payload in sends]
        flat = list(lax.optimization_barrier(tuple(flat)))
        for (k, t), (sends, keeps) in zip(active, plans):
            received = []
            for p in range(len(sends)):
                bit = keeps[p][2]
                pairs = [(q, q ^ (1 << bit)) for q in range(bl_devices)]
                received.append(lax.ppermute(flat.pop(0), "bl", perm=pairs))
            states[k] = fold_step(keeps, received)
            if t == bits - 1:
                summed_modes = jnp.concatenate([states[k][0][0], states[k][1][0]], axis=2)
                if len(pieces) >= 2:
                    summed_modes, pieces[-2] = lax.optimization_barrier((summed_modes, pieces[-2]))
                moved = lax.all_to_all(encode_pairs(summed_modes, 2), "freq", split_axis=0, concat_axis=1, tiled=True)
                owner_modes = decode_pairs(moved, 2)
                lo = k * chunk
                pieces.append(
                    weigh_all(inverse_cov[lo:lo + chunk], noise_power[lo:lo + chunk], owner_modes)
                )
    filtered = jnp.concatenate(pieces, axis=0)
    return filtered.reshape(filtered.shape[:2] + (-1,))


def solution(mesh):
    placed = (
        P(None, None, "freq", "bl"),
        P(),
        P(),
        P(("bl", "freq"), None, None),
        P(("bl", "freq"), None),
    )
    return jax.shard_map(
        body, mesh=mesh, in_specs=placed, out_specs=P(("bl", "freq"), None, None), check_vma=False
    )
```

```python
import math

import jax
import jax.numpy as jnp
from jax import lax
from jax.sharding import PartitionSpec as P

CHUNKS = 4


def dft_table(mode_index, sample_ids, length, chunk_count):
    phase_steps = mode_index[None, :] * sample_ids[:, None] % length
    phases = phase_steps.astype(jnp.float32) * (2.0 * math.pi / length)
    norming = 1.0 / math.sqrt(length)
    cosine = (jnp.cos(phases) * norming).reshape(sample_ids.shape[0], chunk_count, 1, -1)
    sine_part = (jnp.sin(phases) * norming).reshape(sample_ids.shape[0], chunk_count, 1, -1)
    real_rows = jnp.concatenate([cosine, -sine_part], axis=2)
    imag_rows = jnp.concatenate([sine_part, cosine], axis=2)
    table = jnp.stack([real_rows, imag_rows]).astype(jnp.bfloat16)
    return table.reshape(2, sample_ids.shape[0], -1)


def transform(samples, dft_weights):
    return lax.dot_general(
        samples, dft_weights, (((0, 3), (0, 1)), ((), ())), preferred_element_type=jnp.float32
    )


def project(spectrum, beam_rows):
    row_count, freq_count, column_total = spectrum.shape
    mode_count = column_total // 2
    halves = spectrum.reshape(row_count, freq_count, 2, mode_count)
    high = lax.reduce_precision(halves, exponent_bits=8, mantissa_bits=7)
    low = (halves - high).astype(jnp.bfloat16)
    high = high.astype(jnp.bfloat16)
    dims = (((0,), (2,)), ((3,), (0,)))
    projected = lax.dot_general(high, beam_rows, dims, preferred_element_type=jnp.float32)
    projected = projected + lax.dot_general(low, beam_rows, dims, preferred_element_type=jnp.float32)
    return projected


RESIDUAL_LEVELS = 7
RESIDUAL_SCALE = RESIDUAL_LEVELS * 256.0


def encode_pairs(block, axis):
    high = lax.reduce_precision(block, exponent_bits=8, mantissa_bits=7)
    size = jnp.abs(high)
    ratio = jnp.where(size > 0, (block - high) / jnp.where(size > 0, size, 1.0), 0.0)
    steps = jnp.clip(jnp.round(ratio * RESIDUAL_SCALE), -RESIDUAL_LEVELS, RESIDUAL_LEVELS)
    rows = block.shape[axis] // 2
    first = lax.slice_in_dim(steps, 0, rows, axis=axis)
    second = lax.slice_in_dim(steps, rows, 2 * rows, axis=axis)
    code = first * (2 * RESIDUAL_LEVELS + 1) + second
    return jnp.concatenate([high, code], axis=axis).astype(jnp.bfloat16)


def decode_pairs(payload, axis):
    rows = payload.shape[axis] // 3
    high = lax.slice_in_dim(payload, 0, 2 * rows, axis=axis).astype(jnp.float32)
    code = lax.slice_in_dim(payload, 2 * rows, 3 * rows, axis=axis).astype(jnp.float32)
    first = jnp.round(code / (2 * RESIDUAL_LEVELS + 1))
    second = code - first * (2 * RESIDUAL_LEVELS + 1)
    steps = jnp.concatenate([first, second], axis=axis)
    return high + jnp.abs(high) * (steps / RESIDUAL_SCALE)


def split_for_bl(partial, bl_devices):
    bits = bl_devices.bit_length() - 1
    rows = partial.shape[0]
    grid = partial.reshape((2,) * bits + (rows // bl_devices,) + partial.shape[1:])
    return [[grid[..., 0:1, :], [bits - 1 - a for a in range(bits)]],
            [grid[..., 1:2, :], [bits - 1 - a for a in range(bits)]]]


def exchange_step(state, step, bl_devices):
    bits = bl_devices.bit_length() - 1
    orders = [list(range(bits)), list(reversed(range(bits)))]
    sends, keeps = [], []
    for p, (data, axis_bits) in enumerate(state):
        bit = orders[p][step]
        axis = axis_bits.index(bit)
        keeps.append((lax.index_in_dim(data, 0, axis, keepdims=False), axis_bits[:axis] + axis_bits[axis + 1:], bit))
        send = lax.index_in_dim(data, 1, axis, keepdims=False)
        row_axis = len(axis_bits) - 1
        sends.append(encode_pairs(send, row_axis) if send.shape[row_axis] % 2 == 0 else send)
    return sends, keeps


def fold_step(keeps, received):
    state = []
    for (keep, axis_bits, bit), moved in zip(keeps, received):
        row_axis = len(axis_bits)
        if moved.dtype == jnp.bfloat16:
            moved = decode_pairs(moved, row_axis)
        state.append([keep + moved, axis_bits])
    return state


def weigh_all(inverse_cov, noise_power, owner_modes):
    weighted = jnp.einsum("mfg,mgcs->mfcs", inverse_cov, owner_modes, precision=lax.Precision.HIGH)
    return owner_modes - noise_power[:, :, None, None] * weighted


def body(visibility, mode_index, beam_mode_weights, inverse_cov, noise_power):
    bl_devices = lax.axis_size("bl")
    freq_devices = lax.axis_size("freq")
    local_times = visibility.shape[3]
    total_times = local_times * bl_devices
    owned = inverse_cov.shape[0]
    chunk_count = math.gcd(CHUNKS, owned)
    chunk = owned // chunk_count
    me = lax.axis_index("bl")
    sample_ids = me * local_times + jnp.arange(local_times, dtype=jnp.int32)
    owners = jnp.bitwise_xor(me, jnp.arange(bl_devices, dtype=jnp.int32))
    index_grid = jnp.take(
        mode_index.reshape(bl_devices, freq_devices, chunk_count, chunk), owners, axis=0, mode="clip"
    )
    ordered_modes = jnp.transpose(index_grid, (2, 0, 1, 3)).reshape(-1)
    beam_tail = beam_mode_weights.shape[1:]
    beam_grid = jnp.take(
        beam_mode_weights.reshape((bl_devices, freq_devices, chunk_count, chunk) + beam_tail), owners, axis=0,
        mode="clip",
    )
    dft_weights = dft_table(ordered_modes, sample_ids, total_times, chunk_count)
    width = dft_weights.shape[2] // chunk_count
    bits = bl_devices.bit_length() - 1

    def chunk_state(columns, step):
        beams = beam_grid[:, :, step].reshape((-1,) + beam_tail)
        return split_for_bl(project(columns, beams), bl_devices)

    states = [chunk_state(transform(visibility, dft_weights[:, :, :width]), 0)] + [None] * (chunk_count - 1)
    rest_weights = dft_weights[:, :, width:]
    pieces = []
    for slot in range(chunk_count + bits - 1):
        active = [(slot - t, t) for t in range(bits) if 0 <= slot - t < chunk_count]
        plans = [exchange_step(states[k], t, bl_devices) for k, t in active]
        flat = [payload for sends, _ in plans for payload in sends]
        if slot == 0 and chunk_count > 1:
            flat = list(lax.optimization_barrier(tuple(flat) + (rest_weights,)))
            rest_weights = flat.pop()
        else:
            flat = list(lax.optimization_barrier(tuple(flat)))
        for (k, t), (sends, keeps) in zip(active, plans):
            received = []
            for p in range(len(sends)):
                bit = keeps[p][2]
                pairs = [(q, q ^ (1 << bit)) for q in range(bl_devices)]
                received.append(lax.ppermute(flat.pop(0), "bl", perm=pairs))
            states[k] = fold_step(keeps, received)
            if slot == 0 and chunk_count > 1:
                rest = transform(visibility, rest_weights)
                for later in range(1, chunk_count):
                    states[later] = chunk_state(rest[:, :, (later - 1) * width:later * width], later)
            if t == bits - 1:
                summed_modes = jnp.concatenate([states[k][0][0], states[k][1][0]], axis=2)
                if len(pieces) >= 2:
                    summed_modes, pieces[-2] = lax.optimization_barrier((summed_modes, pieces[-2]))
                moved = lax.all_to_all(encode_pairs(summed_modes, 2), "freq", split_axis=0, concat_axis=1, tiled=True)
                owner_modes = decode_pairs(moved, 2)
                lo = k * chunk
                pieces.append(
                    weigh_all(inverse_cov[lo:lo + chunk], noise_power[lo:lo + chunk], owner_modes)
                )
    filtered = jnp.concatenate(pieces, axis=0)
    return filtered.reshape(filtered.shape[:2] + (-1,))


def solution(mesh):
    placed = (
        P(None, None, "freq", "bl"),
        P(),
        P(),
        P(("bl", "freq"), None, None),
        P(("bl", "freq"), None),
    )
    return jax.shard_map(
        body, mesh=mesh, in_specs=placed, out_specs=P(("bl", "freq"), None, None), check_vma=False
    )
```

```python
import math

import jax
import jax.numpy as jnp
from jax import lax
from jax.sharding import PartitionSpec as P

CHUNKS = 4


def dft_table(mode_index, sample_ids, length, chunk_count):
    phase_steps = mode_index[None, :] * sample_ids[:, None] % length
    phases = phase_steps.astype(jnp.float32) * (2.0 * math.pi / length)
    norming = 1.0 / math.sqrt(length)
    cosine = (jnp.cos(phases) * norming).reshape(sample_ids.shape[0], chunk_count, 1, -1)
    sine_part = (jnp.sin(phases) * norming).reshape(sample_ids.shape[0], chunk_count, 1, -1)
    real_rows = jnp.concatenate([cosine, -sine_part], axis=2)
    imag_rows = jnp.concatenate([sine_part, cosine], axis=2)
    table = jnp.stack([real_rows, imag_rows]).astype(jnp.bfloat16)
    return table.reshape(2, sample_ids.shape[0], -1)


def transform(samples, dft_weights):
    return lax.dot_general(
        samples, dft_weights, (((0, 3), (0, 1)), ((), ())), preferred_element_type=jnp.float32
    )


def project(spectrum, beam_rows):
    row_count, freq_count, column_total = spectrum.shape
    mode_count = column_total // 2
    halves = spectrum.reshape(row_count, freq_count, 2, mode_count)
    high = lax.reduce_precision(halves, exponent_bits=8, mantissa_bits=7)
    low = (halves - high).astype(jnp.bfloat16)
    high = high.astype(jnp.bfloat16)
    dims = (((0,), (2,)), ((3,), (0,)))
    projected = lax.dot_general(high, beam_rows, dims, preferred_element_type=jnp.float32)
    projected = projected + lax.dot_general(low, beam_rows, dims, preferred_element_type=jnp.float32)
    return projected


RESIDUAL_LEVELS = 7
RESIDUAL_SCALE = RESIDUAL_LEVELS * 256.0


def encode_pairs(block, axis):
    high = lax.reduce_precision(block, exponent_bits=8, mantissa_bits=7)
    size = jnp.abs(high)
    ratio = jnp.where(size > 0, (block - high) / jnp.where(size > 0, size, 1.0), 0.0)
    steps = jnp.clip(jnp.round(ratio * RESIDUAL_SCALE), -RESIDUAL_LEVELS, RESIDUAL_LEVELS)
    rows = block.shape[axis] // 2
    first = lax.slice_in_dim(steps, 0, rows, axis=axis)
    second = lax.slice_in_dim(steps, rows, 2 * rows, axis=axis)
    code = first * (2 * RESIDUAL_LEVELS + 1) + second
    return jnp.concatenate([high, code], axis=axis).astype(jnp.bfloat16)


def decode_pairs(payload, axis):
    rows = payload.shape[axis] // 3
    high = lax.slice_in_dim(payload, 0, 2 * rows, axis=axis).astype(jnp.float32)
    code = lax.slice_in_dim(payload, 2 * rows, 3 * rows, axis=axis).astype(jnp.float32)
    first = jnp.round(code / (2 * RESIDUAL_LEVELS + 1))
    second = code - first * (2 * RESIDUAL_LEVELS + 1)
    steps = jnp.concatenate([first, second], axis=axis)
    return high + jnp.abs(high) * (steps / RESIDUAL_SCALE)


def split_for_bl(partial, bl_devices):
    bits = bl_devices.bit_length() - 1
    rows = partial.shape[0]
    grid = partial.reshape((2,) * bits + (rows // bl_devices,) + partial.shape[1:])
    return [[grid[..., 0:1, :], [bits - 1 - a for a in range(bits)]],
            [grid[..., 1:2, :], [bits - 1 - a for a in range(bits)]]]


def exchange_step(state, step, bl_devices):
    bits = bl_devices.bit_length() - 1
    orders = [list(range(bits)), list(reversed(range(bits)))]
    sends, keeps = [], []
    for p, (data, axis_bits) in enumerate(state):
        bit = orders[p][step]
        axis = axis_bits.index(bit)
        keeps.append((lax.index_in_dim(data, 0, axis, keepdims=False), axis_bits[:axis] + axis_bits[axis + 1:], bit))
        send = lax.index_in_dim(data, 1, axis, keepdims=False)
        row_axis = len(axis_bits) - 1
        sends.append(encode_pairs(send, row_axis) if send.shape[row_axis] % 2 == 0 else send)
    return sends, keeps


def fold_step(keeps, received):
    state = []
    for (keep, axis_bits, bit), moved in zip(keeps, received):
        row_axis = len(axis_bits)
        if moved.dtype == jnp.bfloat16:
            moved = decode_pairs(moved, row_axis)
        state.append([keep + moved, axis_bits])
    return state


def weigh_all(inverse_cov, noise_power, owner_modes):
    weighted = jnp.einsum("mfg,mgcs->mfcs", inverse_cov, owner_modes, precision=lax.Precision.HIGH)
    return owner_modes - noise_power[:, :, None, None] * weighted


def body(visibility, mode_index, beam_mode_weights, inverse_cov, noise_power):
    bl_devices = lax.axis_size("bl")
    freq_devices = lax.axis_size("freq")
    local_times = visibility.shape[3]
    total_times = local_times * bl_devices
    owned = inverse_cov.shape[0]
    chunk_count = math.gcd(CHUNKS, owned)
    chunk = owned // chunk_count
    me = lax.axis_index("bl")
    sample_ids = me * local_times + jnp.arange(local_times, dtype=jnp.int32)
    owners = jnp.bitwise_xor(me, jnp.arange(bl_devices, dtype=jnp.int32))
    index_grid = jnp.take(
        mode_index.reshape(bl_devices, freq_devices, chunk_count, chunk), owners, axis=0, mode="clip"
    )
    ordered_modes = jnp.transpose(index_grid, (2, 0, 1, 3)).reshape(-1)
    beam_tail = beam_mode_weights.shape[1:]
    beam_grid = jnp.take(
        beam_mode_weights.reshape((bl_devices, freq_devices, chunk_count, chunk) + beam_tail), owners, axis=0,
        mode="clip",
    )
    dft_weights = dft_table(ordered_modes, sample_ids, total_times, chunk_count)
    spectrum = transform(visibility, dft_weights)
    width = spectrum.shape[2] // chunk_count
    bits = bl_devices.bit_length() - 1
    def chunk_inputs(step):
        return spectrum[:, :, step * width:(step + 1) * width], beam_grid[:, :, step].reshape((-1,) + beam_tail)

    def chunk_state(columns, beams):
        return split_for_bl(project(columns, beams), bl_devices)

    states = [chunk_state(*chunk_inputs(0))] + [None] * (chunk_count - 1)
    pieces = []
    for slot in range(chunk_count + bits - 1):
        active = [(slot - t, t) for t in range(bits) if 0 <= slot - t < chunk_count]
        plans = [exchange_step(states[k], t, bl_devices) for k, t in active]
        flat = [payload for sends, _ in plans for payload in sends]
        upcoming = slot + 1 < chunk_count
        if upcoming:
            flat += list(chunk_inputs(slot + 1))
        flat = list(lax.optimization_barrier(tuple(flat)))
        if upcoming:
            beams = flat.pop()
            states[slot + 1] = chunk_state(flat.pop(), beams)
        for (k, t), (sends, keeps) in zip(active, plans):
            received = []
            for p in range(len(sends)):
                bit = keeps[p][2]
                pairs = [(q, q ^ (1 << bit)) for q in range(bl_devices)]
                received.append(lax.ppermute(flat.pop(0), "bl", perm=pairs))
            states[k] = fold_step(keeps, received)
            if t == bits - 1:
                summed_modes = jnp.concatenate([states[k][0][0], states[k][1][0]], axis=2)
                if len(pieces) >= 2:
                    summed_modes, pieces[-2] = lax.optimization_barrier((summed_modes, pieces[-2]))
                moved = lax.all_to_all(encode_pairs(summed_modes, 2), "freq", split_axis=0, concat_axis=1, tiled=True)
                owner_modes = decode_pairs(moved, 2)
                lo = k * chunk
                pieces.append(
                    weigh_all(inverse_cov[lo:lo + chunk], noise_power[lo:lo + chunk], owner_modes)
                )
    filtered = jnp.concatenate(pieces, axis=0)
    return filtered.reshape(filtered.shape[:2] + (-1,))


def solution(mesh):
    placed = (
        P(None, None, "freq", "bl"),
        P(),
        P(),
        P(("bl", "freq"), None, None),
        P(("bl", "freq"), None),
    )
    return jax.shard_map(
        body, mesh=mesh, in_specs=placed, out_specs=P(("bl", "freq"), None, None), check_vma=False
    )
```

```python
import math

import jax
import jax.numpy as jnp
from jax import lax
from jax.sharding import PartitionSpec as P

CHUNKS = 8


def dft_table(mode_index, sample_ids, length, chunk_count):
    phase_steps = mode_index[None, :] * sample_ids[:, None] % length
    phases = phase_steps.astype(jnp.float32) * (2.0 * math.pi / length)
    norming = 1.0 / math.sqrt(length)
    cosine = (jnp.cos(phases) * norming).reshape(sample_ids.shape[0], chunk_count, 1, -1)
    sine_part = (jnp.sin(phases) * norming).reshape(sample_ids.shape[0], chunk_count, 1, -1)
    real_rows = jnp.concatenate([cosine, -sine_part], axis=2)
    imag_rows = jnp.concatenate([sine_part, cosine], axis=2)
    table = jnp.stack([real_rows, imag_rows]).astype(jnp.bfloat16)
    return table.reshape(2, sample_ids.shape[0], -1)


def transform(samples, dft_weights):
    return lax.dot_general(
        samples, dft_weights, (((0, 3), (0, 1)), ((), ())), preferred_element_type=jnp.float32
    )


def project(spectrum, beam_rows):
    row_count, freq_count, column_total = spectrum.shape
    mode_count = column_total // 2
    halves = spectrum.reshape(row_count, freq_count, 2, mode_count)
    high = lax.reduce_precision(halves, exponent_bits=8, mantissa_bits=7)
    low = (halves - high).astype(jnp.bfloat16)
    high = high.astype(jnp.bfloat16)
    dims = (((0,), (2,)), ((3,), (0,)))
    projected = lax.dot_general(high, beam_rows, dims, preferred_element_type=jnp.float32)
    projected = projected + lax.dot_general(low, beam_rows, dims, preferred_element_type=jnp.float32)
    return projected


RESIDUAL_LEVELS = 7
RESIDUAL_SCALE = RESIDUAL_LEVELS * 256.0


def encode_pairs(block, axis):
    high = lax.reduce_precision(block, exponent_bits=8, mantissa_bits=7)
    size = jnp.abs(high)
    ratio = jnp.where(size > 0, (block - high) / jnp.where(size > 0, size, 1.0), 0.0)
    steps = jnp.clip(jnp.round(ratio * RESIDUAL_SCALE), -RESIDUAL_LEVELS, RESIDUAL_LEVELS)
    rows = block.shape[axis] // 2
    first = lax.slice_in_dim(steps, 0, rows, axis=axis)
    second = lax.slice_in_dim(steps, rows, 2 * rows, axis=axis)
    code = first * (2 * RESIDUAL_LEVELS + 1) + second
    return jnp.concatenate([high, code], axis=axis).astype(jnp.bfloat16)


def decode_pairs(payload, axis):
    rows = payload.shape[axis] // 3
    high = lax.slice_in_dim(payload, 0, 2 * rows, axis=axis).astype(jnp.float32)
    code = lax.slice_in_dim(payload, 2 * rows, 3 * rows, axis=axis).astype(jnp.float32)
    first = jnp.round(code / (2 * RESIDUAL_LEVELS + 1))
    second = code - first * (2 * RESIDUAL_LEVELS + 1)
    steps = jnp.concatenate([first, second], axis=axis)
    return high + jnp.abs(high) * (steps / RESIDUAL_SCALE)


def split_for_bl(partial, bl_devices):
    bits = bl_devices.bit_length() - 1
    rows = partial.shape[0]
    grid = partial.reshape((2,) * bits + (rows // bl_devices,) + partial.shape[1:])
    return [[grid[..., 0:1, :], [bits - 1 - a for a in range(bits)]],
            [grid[..., 1:2, :], [bits - 1 - a for a in range(bits)]]]


def exchange_step(state, step, bl_devices):
    bits = bl_devices.bit_length() - 1
    orders = [list(range(bits)), list(reversed(range(bits)))]
    sends, keeps = [], []
    for p, (data, axis_bits) in enumerate(state):
        bit = orders[p][step]
        axis = axis_bits.index(bit)
        keeps.append((lax.index_in_dim(data, 0, axis, keepdims=False), axis_bits[:axis] + axis_bits[axis + 1:], bit))
        send = lax.index_in_dim(data, 1, axis, keepdims=False)
        row_axis = len(axis_bits) - 1
        sends.append(encode_pairs(send, row_axis) if send.shape[row_axis] % 2 == 0 else send)
    return sends, keeps


def fold_step(keeps, received):
    state = []
    for (keep, axis_bits, bit), moved in zip(keeps, received):
        row_axis = len(axis_bits)
        if moved.dtype == jnp.bfloat16:
            moved = decode_pairs(moved, row_axis)
        state.append([keep + moved, axis_bits])
    return state


def weigh_all(inverse_cov, noise_power, owner_modes):
    weighted = jnp.einsum("mfg,mgcs->mfcs", inverse_cov, owner_modes, precision=lax.Precision.HIGH)
    return owner_modes - noise_power[:, :, None, None] * weighted


def body(visibility, mode_index, beam_mode_weights, inverse_cov, noise_power):
    bl_devices = lax.axis_size("bl")
    freq_devices = lax.axis_size("freq")
    local_times = visibility.shape[3]
    total_times = local_times * bl_devices
    owned = inverse_cov.shape[0]
    chunk_count = math.gcd(CHUNKS, owned)
    chunk = owned // chunk_count
    me = lax.axis_index("bl")
    sample_ids = me * local_times + jnp.arange(local_times, dtype=jnp.int32)
    owners = jnp.bitwise_xor(me, jnp.arange(bl_devices, dtype=jnp.int32))
    index_grid = jnp.take(
        mode_index.reshape(bl_devices, freq_devices, chunk_count, chunk), owners, axis=0, mode="clip"
    )
    ordered_modes = jnp.transpose(index_grid, (2, 0, 1, 3)).reshape(-1)
    beam_tail = beam_mode_weights.shape[1:]
    beam_grid = jnp.take(
        beam_mode_weights.reshape((bl_devices, freq_devices, chunk_count, chunk) + beam_tail), owners, axis=0,
        mode="clip",
    )
    dft_weights = dft_table(ordered_modes, sample_ids, total_times, chunk_count)
    spectrum = transform(visibility, dft_weights)
    width = spectrum.shape[2] // chunk_count
    bits = bl_devices.bit_length() - 1
    def chunk_inputs(step):
        return spectrum[:, :, step * width:(step + 1) * width], beam_grid[:, :, step].reshape((-1,) + beam_tail)

    def chunk_state(columns, beams):
        return split_for_bl(project(columns, beams), bl_devices)

    states = [chunk_state(*chunk_inputs(0))] + [None] * (chunk_count - 1)
    pieces = []
    for slot in range(chunk_count + bits - 1):
        active = [(slot - t, t) for t in range(bits) if 0 <= slot - t < chunk_count]
        plans = [exchange_step(states[k], t, bl_devices) for k, t in active]
        flat = [payload for sends, _ in plans for payload in sends]
        upcoming = slot + 1 < chunk_count
        if upcoming:
            flat += list(chunk_inputs(slot + 1))
        flat = list(lax.optimization_barrier(tuple(flat)))
        if upcoming:
            beams = flat.pop()
            states[slot + 1] = chunk_state(flat.pop(), beams)
        for (k, t), (sends, keeps) in zip(active, plans):
            received = []
            for p in range(len(sends)):
                bit = keeps[p][2]
                pairs = [(q, q ^ (1 << bit)) for q in range(bl_devices)]
                received.append(lax.ppermute(flat.pop(0), "bl", perm=pairs))
            states[k] = fold_step(keeps, received)
            if t == bits - 1:
                summed_modes = jnp.concatenate([states[k][0][0], states[k][1][0]], axis=2)
                if len(pieces) >= 2:
                    summed_modes, pieces[-2] = lax.optimization_barrier((summed_modes, pieces[-2]))
                moved = lax.all_to_all(encode_pairs(summed_modes, 2), "freq", split_axis=0, concat_axis=1, tiled=True)
                owner_modes = decode_pairs(moved, 2)
                lo = k * chunk
                pieces.append(
                    weigh_all(inverse_cov[lo:lo + chunk], noise_power[lo:lo + chunk], owner_modes)
                )
    filtered = jnp.concatenate(pieces, axis=0)
    return filtered.reshape(filtered.shape[:2] + (-1,))


def solution(mesh):
    placed = (
        P(None, None, "freq", "bl"),
        P(),
        P(),
        P(("bl", "freq"), None, None),
        P(("bl", "freq"), None),
    )
    return jax.shard_map(
        body, mesh=mesh, in_specs=placed, out_specs=P(("bl", "freq"), None, None), check_vma=False
    )
```

```python
import math

import jax
import jax.numpy as jnp
from jax import lax
from jax.sharding import PartitionSpec as P

CHUNKS = 4


def dft_table(mode_index, sample_ids, length, chunk_count):
    phase_steps = mode_index[None, :] * sample_ids[:, None] % length
    phases = phase_steps.astype(jnp.float32) * (2.0 * math.pi / length)
    norming = 1.0 / math.sqrt(length)
    cosine = (jnp.cos(phases) * norming).reshape(sample_ids.shape[0], chunk_count, 1, -1)
    sine_part = (jnp.sin(phases) * norming).reshape(sample_ids.shape[0], chunk_count, 1, -1)
    real_rows = jnp.concatenate([cosine, -sine_part], axis=2)
    imag_rows = jnp.concatenate([sine_part, cosine], axis=2)
    table = jnp.stack([real_rows, imag_rows]).astype(jnp.bfloat16)
    return table.reshape(2, sample_ids.shape[0], -1)


def transform(samples, dft_weights):
    return lax.dot_general(
        samples, dft_weights, (((0, 3), (0, 1)), ((), ())), preferred_element_type=jnp.float32
    )


def project(spectrum, beam_rows):
    row_count, freq_count, column_total = spectrum.shape
    mode_count = column_total // 2
    halves = spectrum.reshape(row_count, freq_count, 2, mode_count)
    dims = (((0,), (2,)), ((3,), (0,)))
    return lax.dot_general(
        halves, beam_rows.astype(jnp.float32), dims, precision=lax.Precision.HIGH,
        preferred_element_type=jnp.float32,
    )


RESIDUAL_LEVELS = 7
RESIDUAL_SCALE = RESIDUAL_LEVELS * 256.0


def encode_pairs(block, axis):
    high = lax.reduce_precision(block, exponent_bits=8, mantissa_bits=7)
    size = jnp.abs(high)
    ratio = jnp.where(size > 0, (block - high) / jnp.where(size > 0, size, 1.0), 0.0)
    steps = jnp.clip(jnp.round(ratio * RESIDUAL_SCALE), -RESIDUAL_LEVELS, RESIDUAL_LEVELS)
    rows = block.shape[axis] // 2
    first = lax.slice_in_dim(steps, 0, rows, axis=axis)
    second = lax.slice_in_dim(steps, rows, 2 * rows, axis=axis)
    code = first * (2 * RESIDUAL_LEVELS + 1) + second
    return jnp.concatenate([high, code], axis=axis).astype(jnp.bfloat16)


def decode_pairs(payload, axis):
    rows = payload.shape[axis] // 3
    high = lax.slice_in_dim(payload, 0, 2 * rows, axis=axis).astype(jnp.float32)
    code = lax.slice_in_dim(payload, 2 * rows, 3 * rows, axis=axis).astype(jnp.float32)
    first = jnp.round(code / (2 * RESIDUAL_LEVELS + 1))
    second = code - first * (2 * RESIDUAL_LEVELS + 1)
    steps = jnp.concatenate([first, second], axis=axis)
    return high + jnp.abs(high) * (steps / RESIDUAL_SCALE)


def split_for_bl(partial, bl_devices):
    bits = bl_devices.bit_length() - 1
    rows = partial.shape[0]
    grid = partial.reshape((2,) * bits + (rows // bl_devices,) + partial.shape[1:])
    return [[grid[..., 0:1, :], [bits - 1 - a for a in range(bits)]],
            [grid[..., 1:2, :], [bits - 1 - a for a in range(bits)]]]


def exchange_step(state, step, bl_devices):
    bits = bl_devices.bit_length() - 1
    orders = [list(range(bits)), list(reversed(range(bits)))]
    sends, keeps = [], []
    for p, (data, axis_bits) in enumerate(state):
        bit = orders[p][step]
        axis = axis_bits.index(bit)
        keeps.append((lax.index_in_dim(data, 0, axis, keepdims=False), axis_bits[:axis] + axis_bits[axis + 1:], bit))
        send = lax.index_in_dim(data, 1, axis, keepdims=False)
        row_axis = len(axis_bits) - 1
        sends.append(encode_pairs(send, row_axis) if send.shape[row_axis] % 2 == 0 else send)
    return sends, keeps


def fold_step(keeps, received):
    state = []
    for (keep, axis_bits, bit), moved in zip(keeps, received):
        row_axis = len(axis_bits)
        if moved.dtype == jnp.bfloat16:
            moved = decode_pairs(moved, row_axis)
        state.append([keep + moved, axis_bits])
    return state


def weigh_all(inverse_cov, noise_power, owner_modes):
    weighted = jnp.einsum("mfg,mgcs->mfcs", inverse_cov, owner_modes, precision=lax.Precision.HIGH)
    return owner_modes - noise_power[:, :, None, None] * weighted


def body(visibility, mode_index, beam_mode_weights, inverse_cov, noise_power):
    bl_devices = lax.axis_size("bl")
    freq_devices = lax.axis_size("freq")
    local_times = visibility.shape[3]
    total_times = local_times * bl_devices
    owned = inverse_cov.shape[0]
    chunk_count = math.gcd(CHUNKS, owned)
    chunk = owned // chunk_count
    me = lax.axis_index("bl")
    sample_ids = me * local_times + jnp.arange(local_times, dtype=jnp.int32)
    owners = jnp.bitwise_xor(me, jnp.arange(bl_devices, dtype=jnp.int32))
    index_grid = jnp.take(
        mode_index.reshape(bl_devices, freq_devices, chunk_count, chunk), owners, axis=0, mode="clip"
    )
    ordered_modes = jnp.transpose(index_grid, (2, 0, 1, 3)).reshape(-1)
    beam_tail = beam_mode_weights.shape[1:]
    beam_grid = beam_mode_weights.reshape((bl_devices, freq_devices, chunk_count, chunk) + beam_tail)
    dft_weights = dft_table(ordered_modes, sample_ids, total_times, chunk_count)
    spectrum = transform(visibility, dft_weights)
    width = spectrum.shape[2] // chunk_count
    bits = bl_devices.bit_length() - 1
    def chunk_state(step, raw_beams):
        beams = jnp.take(raw_beams, owners, axis=0, mode="clip").reshape((-1,) + beam_tail)
        return split_for_bl(project(spectrum[:, :, step * width:(step + 1) * width], beams), bl_devices)

    states = [chunk_state(0, beam_grid[:, :, 0])] + [None] * (chunk_count - 1)
    pieces = []
    for slot in range(chunk_count + bits - 1):
        active = [(slot - t, t) for t in range(bits) if 0 <= slot - t < chunk_count]
        plans = [exchange_step(states[k], t, bl_devices) for k, t in active]
        flat = [payload for sends, _ in plans for payload in sends]
        upcoming = slot + 1 < chunk_count
        if upcoming:
            flat.append(beam_grid[:, :, slot + 1])
        flat = list(lax.optimization_barrier(tuple(flat)))
        if upcoming:
            states[slot + 1] = chunk_state(slot + 1, flat.pop())
        for (k, t), (sends, keeps) in zip(active, plans):
            received = []
            for p in range(len(sends)):
                bit = keeps[p][2]
                pairs = [(q, q ^ (1 << bit)) for q in range(bl_devices)]
                received.append(lax.ppermute(flat.pop(0), "bl", perm=pairs))
            states[k] = fold_step(keeps, received)
            if t == bits - 1:
                summed_modes = jnp.concatenate([states[k][0][0], states[k][1][0]], axis=2)
                if len(pieces) >= 2:
                    summed_modes, pieces[-2] = lax.optimization_barrier((summed_modes, pieces[-2]))
                moved = lax.all_to_all(encode_pairs(summed_modes, 2), "freq", split_axis=0, concat_axis=1, tiled=True)
                owner_modes = decode_pairs(moved, 2)
                lo = k * chunk
                pieces.append(
                    weigh_all(inverse_cov[lo:lo + chunk], noise_power[lo:lo + chunk], owner_modes)
                )
    filtered = jnp.concatenate(pieces, axis=0)
    return filtered.reshape(filtered.shape[:2] + (-1,))


def solution(mesh):
    placed = (
        P(None, None, "freq", "bl"),
        P(),
        P(),
        P(("bl", "freq"), None, None),
        P(("bl", "freq"), None),
    )
    return jax.shard_map(
        body, mesh=mesh, in_specs=placed, out_specs=P(("bl", "freq"), None, None), check_vma=False
    )
```

```python
import math

import jax
import jax.numpy as jnp
from jax import lax
from jax.sharding import PartitionSpec as P

CHUNKS = 2


def dft_table(mode_index, sample_ids, length, chunk_count):
    phase_steps = mode_index[None, :] * sample_ids[:, None] % length
    phases = phase_steps.astype(jnp.float32) * (2.0 * math.pi / length)
    norming = 1.0 / math.sqrt(length)
    cosine = (jnp.cos(phases) * norming).reshape(sample_ids.shape[0], chunk_count, 1, -1)
    sine_part = (jnp.sin(phases) * norming).reshape(sample_ids.shape[0], chunk_count, 1, -1)
    real_rows = jnp.concatenate([cosine, -sine_part], axis=2)
    imag_rows = jnp.concatenate([sine_part, cosine], axis=2)
    table = jnp.stack([real_rows, imag_rows]).astype(jnp.bfloat16)
    return table.reshape(2, sample_ids.shape[0], -1)


def transform(samples, dft_weights):
    return lax.dot_general(
        samples, dft_weights, (((0, 3), (0, 1)), ((), ())), preferred_element_type=jnp.float32
    )


def project(spectrum, beam_rows):
    row_count, freq_count, column_total = spectrum.shape
    mode_count = column_total // 2
    halves = spectrum.reshape(row_count, freq_count, 2, mode_count)
    high = lax.reduce_precision(halves, exponent_bits=8, mantissa_bits=7)
    low = (halves - high).astype(jnp.bfloat16)
    high = high.astype(jnp.bfloat16)
    dims = (((0,), (2,)), ((3,), (0,)))
    projected = lax.dot_general(high, beam_rows, dims, preferred_element_type=jnp.float32)
    projected = projected + lax.dot_general(low, beam_rows, dims, preferred_element_type=jnp.float32)
    return projected


RESIDUAL_LEVELS = 7
RESIDUAL_SCALE = RESIDUAL_LEVELS * 256.0


def encode_pairs(block, axis):
    high = lax.reduce_precision(block, exponent_bits=8, mantissa_bits=7)
    size = jnp.abs(high)
    ratio = jnp.where(size > 0, (block - high) / jnp.where(size > 0, size, 1.0), 0.0)
    steps = jnp.clip(jnp.round(ratio * RESIDUAL_SCALE), -RESIDUAL_LEVELS, RESIDUAL_LEVELS)
    rows = block.shape[axis] // 2
    first = lax.slice_in_dim(steps, 0, rows, axis=axis)
    second = lax.slice_in_dim(steps, rows, 2 * rows, axis=axis)
    code = first * (2 * RESIDUAL_LEVELS + 1) + second
    return jnp.concatenate([high, code], axis=axis).astype(jnp.bfloat16)


def decode_pairs(payload, axis):
    rows = payload.shape[axis] // 3
    high = lax.slice_in_dim(payload, 0, 2 * rows, axis=axis).astype(jnp.float32)
    code = lax.slice_in_dim(payload, 2 * rows, 3 * rows, axis=axis).astype(jnp.float32)
    first = jnp.round(code / (2 * RESIDUAL_LEVELS + 1))
    second = code - first * (2 * RESIDUAL_LEVELS + 1)
    steps = jnp.concatenate([first, second], axis=axis)
    return high + jnp.abs(high) * (steps / RESIDUAL_SCALE)


def split_for_bl(partial, bl_devices):
    bits = bl_devices.bit_length() - 1
    rows = partial.shape[0]
    grid = partial.reshape((2,) * bits + (rows // bl_devices,) + partial.shape[1:])
    return [[grid[..., 0:1, :], [bits - 1 - a for a in range(bits)]],
            [grid[..., 1:2, :], [bits - 1 - a for a in range(bits)]]]


def exchange_step(state, step, bl_devices):
    bits = bl_devices.bit_length() - 1
    orders = [list(range(bits)), list(reversed(range(bits)))]
    sends, keeps = [], []
    for p, (data, axis_bits) in enumerate(state):
        bit = orders[p][step]
        axis = axis_bits.index(bit)
        keeps.append((lax.index_in_dim(data, 0, axis, keepdims=False), axis_bits[:axis] + axis_bits[axis + 1:], bit))
        send = lax.index_in_dim(data, 1, axis, keepdims=False)
        row_axis = len(axis_bits) - 1
        sends.append(encode_pairs(send, row_axis) if send.shape[row_axis] % 2 == 0 else send)
    return sends, keeps


def fold_step(keeps, received):
    state = []
    for (keep, axis_bits, bit), moved in zip(keeps, received):
        row_axis = len(axis_bits)
        if moved.dtype == jnp.bfloat16:
            moved = decode_pairs(moved, row_axis)
        state.append([keep + moved, axis_bits])
    return state


def weigh_all(inverse_cov, noise_power, owner_modes):
    weighted = jnp.einsum("mfg,mgcs->mfcs", inverse_cov, owner_modes, precision=lax.Precision.HIGH)
    return owner_modes - noise_power[:, :, None, None] * weighted


def body(visibility, mode_index, beam_mode_weights, inverse_cov, noise_power):
    bl_devices = lax.axis_size("bl")
    freq_devices = lax.axis_size("freq")
    local_times = visibility.shape[3]
    total_times = local_times * bl_devices
    owned = inverse_cov.shape[0]
    chunk_count = math.gcd(CHUNKS, owned)
    chunk = owned // chunk_count
    me = lax.axis_index("bl")
    sample_ids = me * local_times + jnp.arange(local_times, dtype=jnp.int32)
    owners = jnp.bitwise_xor(me, jnp.arange(bl_devices, dtype=jnp.int32))
    index_grid = jnp.take(
        mode_index.reshape(bl_devices, freq_devices, chunk_count, chunk), owners, axis=0, mode="clip"
    )
    ordered_modes = jnp.transpose(index_grid, (2, 0, 1, 3)).reshape(-1)
    beam_tail = beam_mode_weights.shape[1:]
    beam_grid = jnp.take(
        beam_mode_weights.reshape((bl_devices, freq_devices, chunk_count, chunk) + beam_tail), owners, axis=0,
        mode="clip",
    )
    dft_weights = dft_table(ordered_modes, sample_ids, total_times, chunk_count)
    spectrum = transform(visibility, dft_weights)
    width = spectrum.shape[2] // chunk_count
    bits = bl_devices.bit_length() - 1
    def chunk_inputs(step):
        return spectrum[:, :, step * width:(step + 1) * width], beam_grid[:, :, step].reshape((-1,) + beam_tail)

    def chunk_state(columns, beams):
        return split_for_bl(project(columns, beams), bl_devices)

    states = [chunk_state(*chunk_inputs(0))] + [None] * (chunk_count - 1)
    pieces = []
    for slot in range(chunk_count + bits - 1):
        active = [(slot - t, t) for t in range(bits) if 0 <= slot - t < chunk_count]
        plans = [exchange_step(states[k], t, bl_devices) for k, t in active]
        flat = [payload for sends, _ in plans for payload in sends]
        upcoming = slot + 1 < chunk_count
        if upcoming:
            flat += list(chunk_inputs(slot + 1))
        flat = list(lax.optimization_barrier(tuple(flat)))
        if upcoming:
            beams = flat.pop()
            states[slot + 1] = chunk_state(flat.pop(), beams)
        for (k, t), (sends, keeps) in zip(active, plans):
            received = []
            for p in range(len(sends)):
                bit = keeps[p][2]
                pairs = [(q, q ^ (1 << bit)) for q in range(bl_devices)]
                received.append(lax.ppermute(flat.pop(0), "bl", perm=pairs))
            states[k] = fold_step(keeps, received)
            if t == bits - 1:
                summed_modes = jnp.concatenate([states[k][0][0], states[k][1][0]], axis=2)
                if len(pieces) >= 2:
                    summed_modes, pieces[-2] = lax.optimization_barrier((summed_modes, pieces[-2]))
                moved = lax.all_to_all(encode_pairs(summed_modes, 2), "freq", split_axis=0, concat_axis=1, tiled=True)
                owner_modes = decode_pairs(moved, 2)
                lo = k * chunk
                pieces.append(
                    weigh_all(inverse_cov[lo:lo + chunk], noise_power[lo:lo + chunk], owner_modes)
                )
    filtered = jnp.concatenate(pieces, axis=0)
    return filtered.reshape(filtered.shape[:2] + (-1,))


def solution(mesh):
    placed = (
        P(None, None, "freq", "bl"),
        P(),
        P(),
        P(("bl", "freq"), None, None),
        P(("bl", "freq"), None),
    )
    return jax.shard_map(
        body, mesh=mesh, in_specs=placed, out_specs=P(("bl", "freq"), None, None), check_vma=False
    )
```

```python
import math

import jax
import jax.numpy as jnp
from jax import lax
from jax.sharding import PartitionSpec as P


def dft_table(mode_index, sample_ids, length, widths):
    phase_steps = mode_index[None, :] * sample_ids[:, None] % length
    phases = phase_steps.astype(jnp.float32) * (2.0 * math.pi / length)
    norming = 1.0 / math.sqrt(length)
    cosine = jnp.cos(phases) * norming
    sine_part = jnp.sin(phases) * norming
    real_cols, imag_cols = [], []
    start = 0
    for width in widths:
        cos_q, sin_q = cosine[:, start:start + width], sine_part[:, start:start + width]
        real_cols += [cos_q, -sin_q]
        imag_cols += [sin_q, cos_q]
        start += width
    return jnp.stack([jnp.concatenate(real_cols, axis=1), jnp.concatenate(imag_cols, axis=1)]).astype(jnp.bfloat16)


def chunk_sizes(owned):
    if owned >= 4 and owned % 2 == 0:
        return [2] * (owned // 2 - 1) + [1, 1]
    return [1] * owned


def transform(samples, dft_weights):
    return lax.dot_general(
        samples, dft_weights, (((0, 3), (0, 1)), ((), ())), preferred_element_type=jnp.float32
    )


def project(spectrum, beam_rows):
    row_count, freq_count, column_total = spectrum.shape
    mode_count = column_total // 2
    halves = spectrum.reshape(row_count, freq_count, 2, mode_count)
    high = lax.reduce_precision(halves, exponent_bits=8, mantissa_bits=7)
    low = (halves - high).astype(jnp.bfloat16)
    high = high.astype(jnp.bfloat16)
    dims = (((0,), (2,)), ((3,), (0,)))
    projected = lax.dot_general(high, beam_rows, dims, preferred_element_type=jnp.float32)
    projected = projected + lax.dot_general(low, beam_rows, dims, preferred_element_type=jnp.float32)
    return projected


RESIDUAL_LEVELS = 7
RESIDUAL_SCALE = RESIDUAL_LEVELS * 256.0


def encode_pairs(block, axis):
    high = lax.reduce_precision(block, exponent_bits=8, mantissa_bits=7)
    size = jnp.abs(high)
    ratio = jnp.where(size > 0, (block - high) / jnp.where(size > 0, size, 1.0), 0.0)
    steps = jnp.clip(jnp.round(ratio * RESIDUAL_SCALE), -RESIDUAL_LEVELS, RESIDUAL_LEVELS)
    rows = block.shape[axis] // 2
    first = lax.slice_in_dim(steps, 0, rows, axis=axis)
    second = lax.slice_in_dim(steps, rows, 2 * rows, axis=axis)
    code = first * (2 * RESIDUAL_LEVELS + 1) + second
    return jnp.concatenate([high, code], axis=axis).astype(jnp.bfloat16)


def decode_pairs(payload, axis):
    rows = payload.shape[axis] // 3
    high = lax.slice_in_dim(payload, 0, 2 * rows, axis=axis).astype(jnp.float32)
    code = lax.slice_in_dim(payload, 2 * rows, 3 * rows, axis=axis).astype(jnp.float32)
    first = jnp.round(code / (2 * RESIDUAL_LEVELS + 1))
    second = code - first * (2 * RESIDUAL_LEVELS + 1)
    steps = jnp.concatenate([first, second], axis=axis)
    return high + jnp.abs(high) * (steps / RESIDUAL_SCALE)


def split_for_bl(partial, bl_devices):
    bits = bl_devices.bit_length() - 1
    rows = partial.shape[0]
    grid = partial.reshape((2,) * bits + (rows // bl_devices,) + partial.shape[1:])
    return [[grid[..., 0:1, :], [bits - 1 - a for a in range(bits)]],
            [grid[..., 1:2, :], [bits - 1 - a for a in range(bits)]]]


def exchange_step(state, step, bl_devices):
    bits = bl_devices.bit_length() - 1
    orders = [list(range(bits)), list(reversed(range(bits)))]
    sends, keeps = [], []
    for p, (data, axis_bits) in enumerate(state):
        bit = orders[p][step]
        axis = axis_bits.index(bit)
        keeps.append((lax.index_in_dim(data, 0, axis, keepdims=False), axis_bits[:axis] + axis_bits[axis + 1:], bit))
        send = lax.index_in_dim(data, 1, axis, keepdims=False)
        row_axis = len(axis_bits) - 1
        sends.append(encode_pairs(send, row_axis) if send.shape[row_axis] % 2 == 0 else send)
    return sends, keeps


def fold_step(keeps, received):
    state = []
    for (keep, axis_bits, bit), moved in zip(keeps, received):
        row_axis = len(axis_bits)
        if moved.dtype == jnp.bfloat16:
            moved = decode_pairs(moved, row_axis)
        state.append([keep + moved, axis_bits])
    return state


def weigh_all(inverse_cov, noise_power, owner_modes):
    weighted = jnp.einsum("mfg,mgcs->mfcs", inverse_cov, owner_modes, precision=lax.Precision.HIGH)
    return owner_modes - noise_power[:, :, None, None] * weighted


def body(visibility, mode_index, beam_mode_weights, inverse_cov, noise_power):
    bl_devices = lax.axis_size("bl")
    freq_devices = lax.axis_size("freq")
    local_times = visibility.shape[3]
    total_times = local_times * bl_devices
    owned = inverse_cov.shape[0]
    sizes = chunk_sizes(owned)
    chunk_count = len(sizes)
    starts = [sum(sizes[:q]) for q in range(chunk_count)]
    group = bl_devices * freq_devices
    me = lax.axis_index("bl")
    sample_ids = me * local_times + jnp.arange(local_times, dtype=jnp.int32)
    owners = jnp.bitwise_xor(me, jnp.arange(bl_devices, dtype=jnp.int32))
    order = []
    for start, size in zip(starts, sizes):
        local = jnp.arange(freq_devices, dtype=jnp.int32)[:, None] * owned + start + jnp.arange(size, dtype=jnp.int32)
        order.append((owners[:, None, None] * (freq_devices * owned) + local[None]).reshape(-1))
    order = jnp.concatenate(order)
    ordered_modes = jnp.take(mode_index, order, mode="clip")
    beam_tail = beam_mode_weights.shape[1:]
    ordered_beams = jnp.take(beam_mode_weights, order, axis=0, mode="clip")
    dft_weights = dft_table(ordered_modes, sample_ids, total_times, [size * group for size in sizes])
    spectrum = transform(visibility, dft_weights)
    bits = bl_devices.bit_length() - 1
    def chunk_inputs(step):
        first, count = starts[step] * group, sizes[step] * group
        return spectrum[:, :, 2 * first:2 * (first + count)], ordered_beams[first:first + count]

    def chunk_state(columns, beams):
        return split_for_bl(project(columns, beams), bl_devices)

    states = [chunk_state(*chunk_inputs(0))] + [None] * (chunk_count - 1)
    pieces = []
    for slot in range(chunk_count + bits - 1):
        active = [(slot - t, t) for t in range(bits) if 0 <= slot - t < chunk_count]
        plans = [exchange_step(states[k], t, bl_devices) for k, t in active]
        flat = [payload for sends, _ in plans for payload in sends]
        upcoming = slot + 1 < chunk_count
        if upcoming:
            flat += list(chunk_inputs(slot + 1))
        flat = list(lax.optimization_barrier(tuple(flat)))
        if upcoming:
            beams = flat.pop()
            states[slot + 1] = chunk_state(flat.pop(), beams)
        for (k, t), (sends, keeps) in zip(active, plans):
            received = []
            for p in range(len(sends)):
                bit = keeps[p][2]
                pairs = [(q, q ^ (1 << bit)) for q in range(bl_devices)]
                received.append(lax.ppermute(flat.pop(0), "bl", perm=pairs))
            states[k] = fold_step(keeps, received)
            if t == bits - 1:
                summed_modes = jnp.concatenate([states[k][0][0], states[k][1][0]], axis=2)
                if len(pieces) >= 2:
                    summed_modes, pieces[-2] = lax.optimization_barrier((summed_modes, pieces[-2]))
                moved = lax.all_to_all(encode_pairs(summed_modes, 2), "freq", split_axis=0, concat_axis=1, tiled=True)
                owner_modes = decode_pairs(moved, 2)
                lo, size = starts[k], sizes[k]
                pieces.append(
                    weigh_all(inverse_cov[lo:lo + size], noise_power[lo:lo + size], owner_modes)
                )
    filtered = jnp.concatenate(pieces, axis=0)
    return filtered.reshape(filtered.shape[:2] + (-1,))


def solution(mesh):
    placed = (
        P(None, None, "freq", "bl"),
        P(),
        P(),
        P(("bl", "freq"), None, None),
        P(("bl", "freq"), None),
    )
    return jax.shard_map(
        body, mesh=mesh, in_specs=placed, out_specs=P(("bl", "freq"), None, None), check_vma=False
    )
```

```python
import math

import jax
import jax.numpy as jnp
from jax import lax
from jax.sharding import PartitionSpec as P

CHUNKS = 4


def dft_table(mode_index, sample_ids, length, chunk_count):
    phase_steps = mode_index[None, :] * sample_ids[:, None] % length
    phases = phase_steps.astype(jnp.float32) * (2.0 * math.pi / length)
    norming = 1.0 / math.sqrt(length)
    cosine = (jnp.cos(phases) * norming).reshape(sample_ids.shape[0], chunk_count, 1, -1)
    sine_part = (jnp.sin(phases) * norming).reshape(sample_ids.shape[0], chunk_count, 1, -1)
    real_rows = jnp.concatenate([cosine, -sine_part], axis=2)
    imag_rows = jnp.concatenate([sine_part, cosine], axis=2)
    table = jnp.stack([real_rows, imag_rows]).astype(jnp.bfloat16)
    return table.reshape(2, sample_ids.shape[0], -1)


def transform(samples, dft_weights):
    return lax.dot_general(
        samples, dft_weights, (((0, 3), (0, 1)), ((), ())), preferred_element_type=jnp.float32
    )


def project(spectrum, beam_rows):
    row_count, freq_count, column_total = spectrum.shape
    mode_count = column_total // 2
    halves = spectrum.reshape(row_count, freq_count, 2, mode_count)
    high = lax.reduce_precision(halves, exponent_bits=8, mantissa_bits=7)
    low = (halves - high).astype(jnp.bfloat16)
    high = high.astype(jnp.bfloat16)
    dims = (((0,), (2,)), ((3,), (0,)))
    projected = lax.dot_general(high, beam_rows, dims, preferred_element_type=jnp.float32)
    projected = projected + lax.dot_general(low, beam_rows, dims, preferred_element_type=jnp.float32)
    return projected


RESIDUAL_LEVELS = 7
RESIDUAL_SCALE = RESIDUAL_LEVELS * 256.0


def encode_pairs(block, axis):
    high = lax.reduce_precision(block, exponent_bits=8, mantissa_bits=7)
    size = jnp.abs(high)
    ratio = jnp.where(size > 0, (block - high) / jnp.where(size > 0, size, 1.0), 0.0)
    steps = jnp.clip(jnp.round(ratio * RESIDUAL_SCALE), -RESIDUAL_LEVELS, RESIDUAL_LEVELS)
    rows = block.shape[axis] // 2
    first = lax.slice_in_dim(steps, 0, rows, axis=axis)
    second = lax.slice_in_dim(steps, rows, 2 * rows, axis=axis)
    code = first * (2 * RESIDUAL_LEVELS + 1) + second
    return jnp.concatenate([high, code], axis=axis).astype(jnp.bfloat16)


def decode_pairs(payload, axis):
    rows = payload.shape[axis] // 3
    high = lax.slice_in_dim(payload, 0, 2 * rows, axis=axis).astype(jnp.float32)
    code = lax.slice_in_dim(payload, 2 * rows, 3 * rows, axis=axis).astype(jnp.float32)
    first = jnp.round(code / (2 * RESIDUAL_LEVELS + 1))
    second = code - first * (2 * RESIDUAL_LEVELS + 1)
    steps = jnp.concatenate([first, second], axis=axis)
    return high + jnp.abs(high) * (steps / RESIDUAL_SCALE)


def split_for_bl(partial, bl_devices):
    bits = bl_devices.bit_length() - 1
    rows = partial.shape[0]
    grid = partial.reshape((2,) * bits + (rows // bl_devices,) + partial.shape[1:])
    return [[grid[..., 0:1, :], [bits - 1 - a for a in range(bits)]],
            [grid[..., 1:2, :], [bits - 1 - a for a in range(bits)]]]


def exchange_step(state, step, bl_devices):
    bits = bl_devices.bit_length() - 1
    orders = [list(range(bits)), list(reversed(range(bits)))]
    sends, keeps = [], []
    for p, (data, axis_bits) in enumerate(state):
        bit = orders[p][step]
        axis = axis_bits.index(bit)
        keeps.append((lax.index_in_dim(data, 0, axis, keepdims=False), axis_bits[:axis] + axis_bits[axis + 1:], bit))
        send = lax.index_in_dim(data, 1, axis, keepdims=False)
        row_axis = len(axis_bits) - 1
        sends.append(encode_pairs(send, row_axis) if send.shape[row_axis] % 2 == 0 else send)
    return sends, keeps


def fold_step(keeps, received):
    state = []
    for (keep, axis_bits, bit), moved in zip(keeps, received):
        row_axis = len(axis_bits)
        if moved.dtype == jnp.bfloat16:
            moved = decode_pairs(moved, row_axis)
        state.append([keep + moved, axis_bits])
    return state


def weigh_all(inverse_cov, noise_power, owner_modes):
    weighted = jnp.einsum("mfg,mgcs->mfcs", inverse_cov, owner_modes, precision=lax.Precision.HIGH)
    return owner_modes - noise_power[:, :, None, None] * weighted


def body(visibility, mode_index, beam_mode_weights, inverse_cov, noise_power):
    bl_devices = lax.axis_size("bl")
    freq_devices = lax.axis_size("freq")
    local_times = visibility.shape[3]
    total_times = local_times * bl_devices
    owned = inverse_cov.shape[0]
    chunk_count = math.gcd(CHUNKS, owned)
    chunk = owned // chunk_count
    me = lax.axis_index("bl")
    sample_ids = me * local_times + jnp.arange(local_times, dtype=jnp.int32)
    owners = jnp.bitwise_xor(me, jnp.arange(bl_devices, dtype=jnp.int32))
    index_grid = jnp.take(
        mode_index.reshape(bl_devices, freq_devices, chunk_count, chunk), owners, axis=0, mode="clip"
    )
    ordered_modes = jnp.transpose(index_grid, (2, 0, 1, 3)).reshape(-1)
    beam_tail = beam_mode_weights.shape[1:]
    beam_grid = jnp.take(
        beam_mode_weights.reshape((bl_devices, freq_devices, chunk_count, chunk) + beam_tail), owners, axis=0,
        mode="clip",
    )
    dft_weights = dft_table(ordered_modes, sample_ids, total_times, chunk_count)
    spectrum = transform(visibility, dft_weights)
    width = spectrum.shape[2] // chunk_count
    bits = bl_devices.bit_length() - 1
    def chunk_inputs(step):
        return spectrum[:, :, step * width:(step + 1) * width], beam_grid[:, :, step].reshape((-1,) + beam_tail)

    def chunk_state(columns, beams):
        return split_for_bl(project(columns, beams), bl_devices)

    states = [chunk_state(*chunk_inputs(0))] + [None] * (chunk_count - 1)
    pieces = []
    for slot in range(chunk_count + bits - 1):
        active = [(slot - t, t) for t in range(bits) if 0 <= slot - t < chunk_count]
        plans = [exchange_step(states[k], t, bl_devices) for k, t in active]
        flat = [payload for sends, _ in plans for payload in sends]
        upcoming = slot + 1 < chunk_count
        if upcoming:
            flat += list(chunk_inputs(slot + 1))
        flat = list(lax.optimization_barrier(tuple(flat)))
        if upcoming:
            beams = flat.pop()
            states[slot + 1] = chunk_state(flat.pop(), beams)
        for (k, t), (sends, keeps) in zip(active, plans):
            received = []
            for p in range(len(sends)):
                bit = keeps[p][2]
                pairs = [(q, q ^ (1 << bit)) for q in range(bl_devices)]
                received.append(lax.ppermute(flat.pop(0), "bl", perm=pairs))
            states[k] = fold_step(keeps, received)
            if t == bits - 1:
                summed_modes = jnp.concatenate([states[k][0][0], states[k][1][0]], axis=2)
                moved = lax.all_to_all(encode_pairs(summed_modes, 2), "freq", split_axis=0, concat_axis=1, tiled=True)
                owner_modes = decode_pairs(moved, 2)
                lo = k * chunk
                pieces.append(
                    weigh_all(inverse_cov[lo:lo + chunk], noise_power[lo:lo + chunk], owner_modes)
                )
    filtered = jnp.concatenate(pieces, axis=0)
    return filtered.reshape(filtered.shape[:2] + (-1,))


def solution(mesh):
    placed = (
        P(None, None, "freq", "bl"),
        P(),
        P(),
        P(("bl", "freq"), None, None),
        P(("bl", "freq"), None),
    )
    return jax.shard_map(
        body, mesh=mesh, in_specs=placed, out_specs=P(("bl", "freq"), None, None), check_vma=False
    )
```

```python
import math

import jax
import jax.numpy as jnp
from jax import lax
from jax.sharding import PartitionSpec as P

CHUNKS = 4


def dft_table(mode_index, sample_ids, length, chunk_count):
    phase_steps = mode_index[None, :] * sample_ids[:, None] % length
    phases = phase_steps.astype(jnp.float32) * (2.0 * math.pi / length)
    norming = 1.0 / math.sqrt(length)
    cosine = (jnp.cos(phases) * norming).reshape(sample_ids.shape[0], chunk_count, 1, -1)
    sine_part = (jnp.sin(phases) * norming).reshape(sample_ids.shape[0], chunk_count, 1, -1)
    real_rows = jnp.concatenate([cosine, -sine_part], axis=2)
    imag_rows = jnp.concatenate([sine_part, cosine], axis=2)
    table = jnp.stack([real_rows, imag_rows]).astype(jnp.bfloat16)
    return table.reshape(2, sample_ids.shape[0], -1)


def transform(samples, dft_weights):
    return lax.dot_general(
        samples, dft_weights, (((0, 3), (0, 1)), ((), ())), preferred_element_type=jnp.float32
    )


def project(spectrum, beam_rows):
    row_count, freq_count, column_total = spectrum.shape
    mode_count = column_total // 2
    halves = spectrum.reshape(row_count, freq_count, 2, mode_count)
    high = lax.reduce_precision(halves, exponent_bits=8, mantissa_bits=7)
    low = (halves - high).astype(jnp.bfloat16)
    high = high.astype(jnp.bfloat16)
    dims = (((0,), (2,)), ((3,), (0,)))
    projected = lax.dot_general(high, beam_rows, dims, preferred_element_type=jnp.float32)
    projected = projected + lax.dot_general(low, beam_rows, dims, preferred_element_type=jnp.float32)
    return projected


RESIDUAL_LEVELS = 7
RESIDUAL_SCALE = RESIDUAL_LEVELS * 256.0


def encode_pairs(block, axis):
    high = lax.reduce_precision(block, exponent_bits=8, mantissa_bits=7)
    size = jnp.abs(high)
    ratio = jnp.where(size > 0, (block - high) / jnp.where(size > 0, size, 1.0), 0.0)
    steps = jnp.clip(jnp.round(ratio * RESIDUAL_SCALE), -RESIDUAL_LEVELS, RESIDUAL_LEVELS)
    rows = block.shape[axis] // 2
    first = lax.slice_in_dim(steps, 0, rows, axis=axis)
    second = lax.slice_in_dim(steps, rows, 2 * rows, axis=axis)
    code = first * (2 * RESIDUAL_LEVELS + 1) + second
    return jnp.concatenate([high, code], axis=axis).astype(jnp.bfloat16)


def decode_pairs(payload, axis):
    rows = payload.shape[axis] // 3
    high = lax.slice_in_dim(payload, 0, 2 * rows, axis=axis).astype(jnp.float32)
    code = lax.slice_in_dim(payload, 2 * rows, 3 * rows, axis=axis).astype(jnp.float32)
    first = jnp.round(code / (2 * RESIDUAL_LEVELS + 1))
    second = code - first * (2 * RESIDUAL_LEVELS + 1)
    steps = jnp.concatenate([first, second], axis=axis)
    return high + jnp.abs(high) * (steps / RESIDUAL_SCALE)


def split_for_bl(partial, bl_devices):
    bits = bl_devices.bit_length() - 1
    rows = partial.shape[0]
    grid = partial.reshape((2,) * bits + (rows // bl_devices,) + partial.shape[1:])
    return [[grid[..., 0:1, :], [bits - 1 - a for a in range(bits)]],
            [grid[..., 1:2, :], [bits - 1 - a for a in range(bits)]]]


def exchange_step(state, step, bl_devices):
    bits = bl_devices.bit_length() - 1
    orders = [list(range(bits)), list(reversed(range(bits)))]
    sends, keeps = [], []
    for p, (data, axis_bits) in enumerate(state):
        bit = orders[p][step]
        axis = axis_bits.index(bit)
        keeps.append((lax.index_in_dim(data, 0, axis, keepdims=False), axis_bits[:axis] + axis_bits[axis + 1:], bit))
        send = lax.index_in_dim(data, 1, axis, keepdims=False)
        row_axis = len(axis_bits) - 1
        sends.append(encode_pairs(send, row_axis) if send.shape[row_axis] % 2 == 0 else send)
    return sends, keeps


def fold_step(keeps, received):
    state = []
    for (keep, axis_bits, bit), moved in zip(keeps, received):
        row_axis = len(axis_bits)
        if moved.dtype == jnp.bfloat16:
            moved = decode_pairs(moved, row_axis)
        state.append([keep + moved, axis_bits])
    return state


def weigh_all(inverse_cov, noise_power, owner_modes):
    weighted = jnp.einsum("mfg,mgcs->mfcs", inverse_cov, owner_modes, precision=lax.Precision.HIGH)
    return owner_modes - noise_power[:, :, None, None] * weighted


def body(visibility, mode_index, beam_mode_weights, inverse_cov, noise_power):
    bl_devices = lax.axis_size("bl")
    freq_devices = lax.axis_size("freq")
    local_times = visibility.shape[3]
    total_times = local_times * bl_devices
    owned = inverse_cov.shape[0]
    chunk_count = math.gcd(CHUNKS, owned)
    chunk = owned // chunk_count
    me = lax.axis_index("bl")
    sample_ids = me * local_times + jnp.arange(local_times, dtype=jnp.int32)
    owners = jnp.bitwise_xor(me, jnp.arange(bl_devices, dtype=jnp.int32))
    index_grid = jnp.take(
        mode_index.reshape(bl_devices, freq_devices, chunk_count, chunk), owners, axis=0, mode="clip"
    )
    ordered_modes = jnp.transpose(index_grid, (2, 0, 1, 3)).reshape(-1)
    beam_tail = beam_mode_weights.shape[1:]
    beam_grid = jnp.take(
        beam_mode_weights.reshape((bl_devices, freq_devices, chunk_count, chunk) + beam_tail), owners, axis=0,
        mode="clip",
    )
    dft_weights = dft_table(ordered_modes, sample_ids, total_times, chunk_count)
    spectrum = transform(visibility, dft_weights)
    width = spectrum.shape[2] // chunk_count
    bits = bl_devices.bit_length() - 1
    def chunk_inputs(step):
        return spectrum, beam_grid[:, :, step].reshape((-1,) + beam_tail)

    def chunk_state(source, beams, step):
        return split_for_bl(project(source[:, :, step * width:(step + 1) * width], beams), bl_devices)

    states = [chunk_state(*chunk_inputs(0), 0)] + [None] * (chunk_count - 1)
    pieces = []
    for slot in range(chunk_count + bits - 1):
        active = [(slot - t, t) for t in range(bits) if 0 <= slot - t < chunk_count]
        plans = [exchange_step(states[k], t, bl_devices) for k, t in active]
        flat = [payload for sends, _ in plans for payload in sends]
        upcoming = slot + 1 < chunk_count
        if upcoming:
            flat += list(chunk_inputs(slot + 1))
        flat = list(lax.optimization_barrier(tuple(flat)))
        if upcoming:
            beams = flat.pop()
            states[slot + 1] = chunk_state(flat.pop(), beams, slot + 1)
        for (k, t), (sends, keeps) in zip(active, plans):
            received = []
            for p in range(len(sends)):
                bit = keeps[p][2]
                pairs = [(q, q ^ (1 << bit)) for q in range(bl_devices)]
                received.append(lax.ppermute(flat.pop(0), "bl", perm=pairs))
            states[k] = fold_step(keeps, received)
            if t == bits - 1:
                summed_modes = jnp.concatenate([states[k][0][0], states[k][1][0]], axis=2)
                moved = lax.all_to_all(encode_pairs(summed_modes, 2), "freq", split_axis=0, concat_axis=1, tiled=True)
                owner_modes = decode_pairs(moved, 2)
                lo = k * chunk
                pieces.append(
                    weigh_all(inverse_cov[lo:lo + chunk], noise_power[lo:lo + chunk], owner_modes)
                )
    filtered = jnp.concatenate(pieces, axis=0)
    return filtered.reshape(filtered.shape[:2] + (-1,))


def solution(mesh):
    placed = (
        P(None, None, "freq", "bl"),
        P(),
        P(),
        P(("bl", "freq"), None, None),
        P(("bl", "freq"), None),
    )
    return jax.shard_map(
        body, mesh=mesh, in_specs=placed, out_specs=P(("bl", "freq"), None, None), check_vma=False
    )
```
